32 devices in a mesh: grp: 8 (over z, x), leaf: 4 (over y, core).
Axes of the slice: x: 2, y: 2, z: 4, core: 2. Of those that a mesh axis runs over, the one named last changes fastest.
Arguments:
- inputs: float32 [65536, 64], P(('grp', 'leaf')), may hold values from -6 to 6
- freqs: float32 [64, 256], replicated, may hold values from -0.75 to 0.75
- phases: float32 [256], replicated, may hold values from -3.140625 to 3.140625
- sample_weight: float32 [65536], P(('grp', 'leaf')), as said below
- stored: float32 [32, 256, 256], P(('grp', 'leaf')), as said below
- root: int32 [32], replicated, may hold values from 0 to 31, each once
Outputs:
- factor: float32 [256, 256], replicated
- basis: float32 [65536, 256], P(('grp', 'leaf'))
The draws below stay inside these ranges and needn't reach their ends.
Inputs may be any that keep to these rules, and one draw needn't show every extreme that they name: `root`: each device index once, in the order grp first, leaf second; only the first entry is read. `stored`: each slot is upper triangular with a positive diagonal. `sample_weight`: positive row weights.
All inputs are finite; a program needn't handle non-finite values.
Results may differ from the reference program's by a relative error of at most 0.0003.
Values sent between devices are 32-bit elements; how exact they have to be, the bound alone decides.
No kernel may reach another device: no remote copies, remote signals or barrier semaphores. Data moves between devices by JAX's collectives and lax.ppermute only.
A program may use at most 64 MiB of HBM per device.

```python
import math
import jax
import jax.numpy as jnp
from jax import lax

IN_DIM = 64
FEATS = 256
ROWS_DEV = 2048
SLOTS = 32
ROWS = 65536


def draw_sample_weight(key, part):
    position = jnp.arange(ROWS).astype(jnp.float32) / ROWS
    rise = jnp.exp(math.log(3.0) * position)
    noise = jnp.exp(jax.random.uniform(key, (ROWS,), jnp.float32, -math.log(3.0), math.log(3.0)))
    return (rise * noise).astype(jnp.float32)


def draw_stored(key, part):
    key_diag = jax.random.fold_in(key, 11)
    key_off = jax.random.fold_in(key, 12)
    diag = jnp.exp(jax.random.uniform(key_diag, (SLOTS, FEATS), jnp.float32, math.log(0.2), math.log(2.0)))
    off = jax.random.uniform(key_off, (SLOTS, FEATS, FEATS), jnp.float32, -1.0, 1.0) * 0.5
    row_idx = jnp.arange(FEATS)[:, None]
    col_idx = jnp.arange(FEATS)[None, :]
    upper = (col_idx > row_idx).astype(jnp.float32)
    eye = (col_idx == row_idx).astype(jnp.float32)
    scaled = off * diag[:, :, None] / math.sqrt(FEATS) * upper[None, :, :]
    return (scaled + diag[:, :, None] * eye[None, :, :]).astype(jnp.float32)


def levels(stream_key, shape, split, low, high):
    def one(axis_at, parts):
        steps = jax.random.uniform(jax.random.fold_in(jax.random.fold_in(stream_key, 6), axis_at), (parts,), jnp.float32, low / len(split), high / len(split))
        return jnp.repeat(jnp.exp(steps), shape[axis_at] // parts).reshape((-1,) + (1,) * (len(shape) - axis_at - 1))

    factor_of = one(*split[0])
    for cut in split[1:]:
        factor_of = factor_of * one(*cut)
    return factor_of


def scatter_about(key, extent, width, reach, shards=(), dtype=jnp.bfloat16):
    entries = width * jax.random.normal(key, extent, jnp.float32)
    if shards:
        entries = entries * levels(key, extent, shards, -0.22, 0.18)
    return jnp.clip(entries, -reach, reach).astype(dtype)


def setup_inputs(seed: int = 0) -> dict:
    seeds = jax.random.split(jax.random.key(seed), 7)
    return {
        "inputs": scatter_about(seeds[0], (ROWS, IN_DIM), 1.0, 6.0, ((0, 32),), jnp.float32),
        "freqs": scatter_about(seeds[1], (IN_DIM, FEATS), IN_DIM ** -0.5, 0.75, (), jnp.float32),
        "phases": jnp.clip(jax.random.uniform(seeds[2], (FEATS,), jnp.float32, -3.140625, 3.140625), -3.140625, 3.140625),
        "sample_weight": draw_sample_weight(jax.random.fold_in(seeds[6], 71), 0),
        "stored": draw_stored(jax.random.fold_in(seeds[6], 71), 0),
        "root": jax.random.permutation(seeds[5], SLOTS).astype(jnp.int32),
    }


def make_features(inputs, freqs, phases, sample_weight):
    proj = jnp.dot(inputs, freqs, precision=lax.Precision.HIGHEST) + phases[None, :]
    return jnp.sqrt(sample_weight)[:, None] * jnp.cos(proj) / jnp.sqrt(jnp.float32(ROWS))

def reference(inputs, freqs, phases, sample_weight, stored, root):
    blocks_in = inputs.reshape(SLOTS, ROWS_DEV, IN_DIM)
    blocks_w = sample_weight.reshape(SLOTS, ROWS_DEV)

    def block_gram(pair):
        feats = make_features(pair[0], freqs, phases, pair[1])
        return jnp.dot(feats.T, feats, precision=lax.Precision.HIGHEST)

    def accumulate(total, pair):
        return (total + block_gram(pair), None)
    running = lax.dynamic_index_in_dim(stored, root[0].astype(jnp.int32), 0, keepdims=False)
    start = jnp.dot(running.T, running, precision=lax.Precision.HIGHEST)
    gram, unused = lax.scan(accumulate, start, (blocks_in, blocks_w))
    lower = jnp.linalg.cholesky(gram)
    factor = lower.T

    def block_basis(pair):
        feats = make_features(pair[0], freqs, phases, pair[1])
        solved = jax.scipy.linalg.solve_triangular(lower, feats.T, lower=True)
        return solved.T * jnp.sqrt(jnp.float32(ROWS))
    basis = lax.map(block_basis, (blocks_in, blocks_w)).reshape(ROWS, FEATS)
    return (factor, basis)
```

```python
import math

import jax
import jax.numpy as jnp
from jax import lax
from jax.sharding import PartitionSpec as P


def partner(array, axis, distance):
    return lax.ppermute(array, axis, [(i, i ^ 1 << distance) for i in range(lax.axis_size(axis))])


def per_device(inputs, freqs, phases, sample_weight, stored, root):
    total_rows = inputs.shape[0] * lax.axis_size("grp") * lax.axis_size("leaf")
    norm_scale = 1.0 / math.sqrt(total_rows)
    proj = jnp.dot(inputs, freqs, precision=lax.Precision.HIGHEST) + phases[None, :]
    features = jnp.sqrt(sample_weight)[:, None] * jnp.cos(proj) * norm_scale
    gram = lax.dot_general(
        features, features, (((0,), (0,)), ((), ())), precision=lax.Precision.HIGHEST
    )
    slot = lax.axis_index("grp") * lax.axis_size("leaf") + lax.axis_index("leaf")
    running = jnp.where(slot == root[0], stored[0], jnp.zeros_like(stored[0]))
    gram = gram + lax.dot_general(
        running, running, (((0,), (0,)), ((), ())), precision=lax.Precision.HIGHEST
    )
    payload = gram
    for bit_leaf in range(lax.axis_size("leaf").bit_length() - 1):
        payload = payload + partner(payload, "leaf", bit_leaf)
    for bit_grp in range(lax.axis_size("grp").bit_length() - 1):
        payload = payload + partner(payload, "grp", bit_grp)
    gram = payload
    lower = jnp.linalg.cholesky(gram)
    solved = jax.scipy.linalg.solve_triangular(lower, features.T, lower=True)
    basis = solved.T * math.sqrt(total_rows)
    return (lower.T, basis)


def solution(mesh):
    return jax.shard_map(
        per_device,
        mesh=mesh,
        in_specs=(
            P(("grp", "leaf"), None),
            P(),
            P(),
            P(("grp", "leaf")),
            P(("grp", "leaf"), None, None),
            P(),
        ),
        out_specs=(P(), P(("grp", "leaf"), None)),
        check_vma=False,
    )
```

```python
import math

import jax
import jax.numpy as jnp
from jax import lax
from jax.sharding import PartitionSpec as P


def partner(array, axis, distance):
    return lax.ppermute(array, axis, [(i, i ^ 1 << distance) for i in range(lax.axis_size(axis))])


def mm(a, b):
    return jnp.dot(a, b, precision=lax.Precision.HIGHEST)


def cholesky_and_inverse(gram):
    n = gram.shape[0]
    h = n // 2
    eye = jnp.eye(h, dtype=gram.dtype)
    l11 = jnp.linalg.cholesky(gram[:h, :h])
    i11 = jax.scipy.linalg.solve_triangular(l11, eye, lower=True)
    l21 = mm(gram[h:, :h], i11.T)
    l22 = jnp.linalg.cholesky(gram[h:, h:] - mm(l21, l21.T))
    i22 = jax.scipy.linalg.solve_triangular(l22, eye, lower=True)
    i21 = -mm(i22, mm(l21, i11))
    zero = jnp.zeros_like(l11)
    lower = jnp.block([[l11, zero], [l21, l22]])
    inverse = jnp.block([[i11, zero], [i21, i22]])
    return lower, inverse


def per_device(inputs, freqs, phases, sample_weight, stored, root):
    total_rows = inputs.shape[0] * lax.axis_size("grp") * lax.axis_size("leaf")
    norm_scale = 1.0 / math.sqrt(total_rows)
    proj = jnp.dot(inputs, freqs, precision=lax.Precision.HIGHEST) + phases[None, :]
    features = jnp.sqrt(sample_weight)[:, None] * jnp.cos(proj) * norm_scale
    gram = lax.dot_general(
        features, features, (((0,), (0,)), ((), ())), precision=lax.Precision.HIGHEST
    )
    slot = lax.axis_index("grp") * lax.axis_size("leaf") + lax.axis_index("leaf")
    running = jnp.where(slot == root[0], stored[0], jnp.zeros_like(stored[0]))
    gram = gram + lax.dot_general(
        running, running, (((0,), (0,)), ((), ())), precision=lax.Precision.HIGHEST
    )
    payload = gram
    for bit_leaf in range(lax.axis_size("leaf").bit_length() - 1):
        payload = payload + partner(payload, "leaf", bit_leaf)
    for bit_grp in range(lax.axis_size("grp").bit_length() - 1):
        payload = payload + partner(payload, "grp", bit_grp)
    gram = payload
    lower, inverse = cholesky_and_inverse(gram)
    basis = lax.dot_general(
        features, inverse, (((1,), (1,)), ((), ())), precision=lax.Precision.HIGHEST
    ) * math.sqrt(total_rows)
    return (lower.T, basis)


def solution(mesh):
    return jax.shard_map(
        per_device,
        mesh=mesh,
        in_specs=(
            P(("grp", "leaf"), None),
            P(),
            P(),
            P(("grp", "leaf")),
            P(("grp", "leaf"), None, None),
            P(),
        ),
        out_specs=(P(), P(("grp", "leaf"), None)),
        check_vma=False,
    )
```

```python
import math

import jax
import jax.numpy as jnp
from jax import lax
from jax.sharding import PartitionSpec as P


def partner(array, axis, distance):
    return lax.ppermute(array, axis, [(i, i ^ 1 << distance) for i in range(lax.axis_size(axis))])


def mm(a, b):
    return jnp.dot(a, b, precision=lax.Precision.HIGHEST)


def cholesky_and_inverse(g11, g21, g22):
    h = g11.shape[0]
    eye = jnp.eye(h, dtype=g11.dtype)
    l11 = jnp.linalg.cholesky(g11)
    i11 = jax.scipy.linalg.solve_triangular(l11, eye, lower=True)
    l21 = mm(g21, i11.T)
    l22 = jnp.linalg.cholesky(g22 - mm(l21, l21.T))
    i22 = jax.scipy.linalg.solve_triangular(l22, eye, lower=True)
    i21 = -mm(i22, mm(l21, i11))
    zero = jnp.zeros_like(l11)
    lower = jnp.block([[l11, zero], [l21, l22]])
    inverse = jnp.block([[i11, zero], [i21, i22]])
    return lower, inverse


def pack(gram):
    h = gram.shape[0] // 2
    row = lax.broadcasted_iota(jnp.int32, (h, h), 0)
    col = lax.broadcasted_iota(jnp.int32, (h, h), 1)
    tri = jnp.where(row <= col, gram[:h, :h], gram[h:, h:])
    diag = jnp.diagonal(gram[h:, h:])
    pad = jnp.zeros((7, h), gram.dtype)
    first = jnp.concatenate([tri, diag[None, :], pad], axis=0)
    second = jnp.concatenate([gram[h:, :h], jnp.zeros((8, h), gram.dtype)], axis=0)
    return first, second


def unpack(first, second):
    h = first.shape[1]
    row = lax.broadcasted_iota(jnp.int32, (h, h), 0)
    col = lax.broadcasted_iota(jnp.int32, (h, h), 1)
    tri = first[:h]
    g11 = jnp.where(row <= col, tri, tri.T)
    g22 = jnp.where(row > col, tri, tri.T)
    g22 = jnp.where(row == col, first[h:h + 1, :], g22)
    g21 = second[:h]
    return g11, g21, g22


def all_reduce_symmetric(gram):
    stages = [("leaf", b) for b in range(lax.axis_size("leaf").bit_length() - 1)]
    stages += [("grp", b) for b in range(lax.axis_size("grp").bit_length() - 1)]
    first, second = pack(gram)
    if not stages:
        return unpack(first, second)
    axis0, bit0 = stages[0]
    low = (lax.axis_index(axis0) >> bit0) % 2 == 0
    keep = jnp.where(low, first, second)
    send = jnp.where(low, second, first)
    keep = keep + partner(send, axis0, bit0)
    for axis, bit in stages[1:]:
        keep = keep + partner(keep, axis, bit)
    other = partner(keep, axis0, bit0)
    first = jnp.where(low, keep, other)
    second = jnp.where(low, other, keep)
    return unpack(first, second)


def per_device(inputs, freqs, phases, sample_weight, stored, root):
    total_rows = inputs.shape[0] * lax.axis_size("grp") * lax.axis_size("leaf")
    norm_scale = 1.0 / math.sqrt(total_rows)
    proj = jnp.dot(inputs, freqs, precision=lax.Precision.HIGHEST) + phases[None, :]
    features = jnp.sqrt(sample_weight)[:, None] * jnp.cos(proj) * norm_scale
    gram = lax.dot_general(
        features, features, (((0,), (0,)), ((), ())), precision=lax.Precision.HIGHEST
    )
    slot = lax.axis_index("grp") * lax.axis_size("leaf") + lax.axis_index("leaf")
    running = jnp.where(slot == root[0], stored[0], jnp.zeros_like(stored[0]))
    gram = gram + lax.dot_general(
        running, running, (((0,), (0,)), ((), ())), precision=lax.Precision.HIGHEST
    )
    gram = all_reduce_symmetric(gram)
    lower, inverse = cholesky_and_inverse(*gram)
    basis = lax.dot_general(
        features, inverse, (((1,), (1,)), ((), ())), precision=lax.Precision.HIGHEST
    ) * math.sqrt(total_rows)
    return (lower.T, basis)


def solution(mesh):
    return jax.shard_map(
        per_device,
        mesh=mesh,
        in_specs=(
            P(("grp", "leaf"), None),
            P(),
            P(),
            P(("grp", "leaf")),
            P(("grp", "leaf"), None, None),
            P(),
        ),
        out_specs=(P(), P(("grp", "leaf"), None)),
        check_vma=False,
    )
```

```python
import math

import jax
import jax.numpy as jnp
from jax import lax
from jax.experimental import pallas as pl
from jax.experimental.pallas import tpu as pltpu
from jax.sharding import PartitionSpec as P


def partner(array, axis, distance):
    return lax.ppermute(array, axis, [(i, i ^ 1 << distance) for i in range(lax.axis_size(axis))])


def mm(a, b):
    return jnp.dot(a, b, precision=lax.Precision.HIGHEST)


def _chol_kernel(g_ref, r_ref, li_ref, a_ref, z_ref):
    n = g_ref.shape[0]
    h = n // 2
    a_ref[...] = g_ref[...]
    row = lax.broadcasted_iota(jnp.int32, (n, n), 0)
    col = lax.broadcasted_iota(jnp.int32, (n, n), 1)
    z_ref[...] = jnp.where(row == col, 1.0, 0.0).astype(jnp.float32)
    lane = lax.broadcasted_iota(jnp.int32, (1, n), 1)

    def step(j, lo):
        a_row = a_ref[pl.ds(j, 1), :]
        d = jnp.sum(jnp.where(lane == j, a_row, 0.0), axis=1, keepdims=True)
        s = 1.0 / jnp.sqrt(d)
        r = jnp.where(lane >= j, a_row * s, 0.0)
        z = z_ref[pl.ds(j, 1), :] * s
        r_ref[pl.ds(j, 1), :] = r
        li_ref[pl.ds(j, 1), :] = z
        c = jnp.broadcast_to(r, (8, n)).T[:, 0:1]
        if lo:
            a_ref[...] = a_ref[...] - c * r
            z_ref[:, :h] = z_ref[:, :h] - c * z[:, :h]
        else:
            a_ref[h:, h:] = a_ref[h:, h:] - c[h:] * r[:, h:]
            z_ref[h:, :] = z_ref[h:, :] - c[h:] * z

    def body_lo(j, carry):
        step(j, True)
        return carry

    def body_hi(j, carry):
        step(j, False)
        return carry

    lax.fori_loop(0, h, body_lo, 0)
    lax.fori_loop(h, n, body_hi, 0)


def cholesky_kernel(gram):
    n = gram.shape[0]
    return pl.pallas_call(
        _chol_kernel,
        out_shape=(jax.ShapeDtypeStruct((n, n), jnp.float32),) * 2,
        in_specs=[pl.BlockSpec(memory_space=pltpu.VMEM)],
        out_specs=(pl.BlockSpec(memory_space=pltpu.VMEM),) * 2,
        scratch_shapes=[pltpu.VMEM((n, n), jnp.float32)] * 2,
    )(gram)


def pack(gram):
    h = gram.shape[0] // 2
    row = lax.broadcasted_iota(jnp.int32, (h, h), 0)
    col = lax.broadcasted_iota(jnp.int32, (h, h), 1)
    tri = jnp.where(row <= col, gram[:h, :h], gram[h:, h:])
    diag = jnp.diagonal(gram[h:, h:])
    pad = jnp.zeros((7, h), gram.dtype)
    first = jnp.concatenate([tri, diag[None, :], pad], axis=0)
    second = jnp.concatenate([gram[h:, :h], jnp.zeros((8, h), gram.dtype)], axis=0)
    return first, second


def unpack(first, second):
    h = first.shape[1]
    row = lax.broadcasted_iota(jnp.int32, (h, h), 0)
    col = lax.broadcasted_iota(jnp.int32, (h, h), 1)
    tri = first[:h]
    g11 = jnp.where(row <= col, tri, tri.T)
    g22 = jnp.where(row > col, tri, tri.T)
    g22 = jnp.where(row == col, first[h:h + 1, :], g22)
    g21 = second[:h]
    return g11, g21, g22


def all_reduce_symmetric(gram):
    stages = [("leaf", b) for b in range(lax.axis_size("leaf").bit_length() - 1)]
    stages += [("grp", b) for b in range(lax.axis_size("grp").bit_length() - 1)]
    first, second = pack(gram)
    if not stages:
        return unpack(first, second)
    axis0, bit0 = stages[0]
    low = (lax.axis_index(axis0) >> bit0) % 2 == 0
    keep = jnp.where(low, first, second)
    send = jnp.where(low, second, first)
    keep = keep + partner(send, axis0, bit0)
    for axis, bit in stages[1:]:
        keep = keep + partner(keep, axis, bit)
    other = partner(keep, axis0, bit0)
    first = jnp.where(low, keep, other)
    second = jnp.where(low, other, keep)
    return unpack(first, second)


def per_device(inputs, freqs, phases, sample_weight, stored, root):
    total_rows = inputs.shape[0] * lax.axis_size("grp") * lax.axis_size("leaf")
    norm_scale = 1.0 / math.sqrt(total_rows)
    proj = jnp.dot(inputs, freqs, precision=lax.Precision.HIGHEST) + phases[None, :]
    features = jnp.sqrt(sample_weight)[:, None] * jnp.cos(proj) * norm_scale
    gram = lax.dot_general(
        features, features, (((0,), (0,)), ((), ())), precision=lax.Precision.HIGHEST
    )
    slot = lax.axis_index("grp") * lax.axis_size("leaf") + lax.axis_index("leaf")
    running = jnp.where(slot == root[0], stored[0], jnp.zeros_like(stored[0]))
    gram = gram + lax.dot_general(
        running, running, (((0,), (0,)), ((), ())), precision=lax.Precision.HIGHEST
    )
    gram = all_reduce_symmetric(gram)
    g11, g21, g22 = gram
    full = jnp.concatenate(
        [jnp.concatenate([g11, g21.T], axis=1), jnp.concatenate([g21, g22], axis=1)], axis=0
    )
    upper, inverse = cholesky_kernel(full)
    basis = lax.dot_general(
        features, inverse, (((1,), (1,)), ((), ())), precision=lax.Precision.HIGHEST
    ) * math.sqrt(total_rows)
    return (upper, basis)


def solution(mesh):
    return jax.shard_map(
        per_device,
        mesh=mesh,
        in_specs=(
            P(("grp", "leaf"), None),
            P(),
            P(),
            P(("grp", "leaf")),
            P(("grp", "leaf"), None, None),
            P(),
        ),
        out_specs=(P(), P(("grp", "leaf"), None)),
        check_vma=False,
    )
```

```python
import math

import jax
import jax.numpy as jnp
from jax import lax
from jax.sharding import PartitionSpec as P


def partner(array, axis, distance):
    return lax.ppermute(array, axis, [(i, i ^ 1 << distance) for i in range(lax.axis_size(axis))])


def mm(a, b):
    return jnp.dot(a, b, precision=lax.Precision.HIGHEST)


def cholesky_and_inverse(g11, g21, g22):
    h = g11.shape[0]
    eye = jnp.eye(h, dtype=g11.dtype)
    l11 = jnp.linalg.cholesky(g11)
    i11 = jax.scipy.linalg.solve_triangular(l11, eye, lower=True)
    l21 = mm(g21, i11.T)
    l22 = jnp.linalg.cholesky(g22 - mm(l21, l21.T))
    i22 = jax.scipy.linalg.solve_triangular(l22, eye, lower=True)
    i21 = -mm(i22, mm(l21, i11))
    zero = jnp.zeros_like(l11)
    lower = jnp.block([[l11, zero], [l21, l22]])
    inverse = jnp.block([[i11, zero], [i21, i22]])
    return lower, inverse


def pack(gram):
    h = gram.shape[0] // 2
    row = lax.broadcasted_iota(jnp.int32, (h, h), 0)
    col = lax.broadcasted_iota(jnp.int32, (h, h), 1)
    tri = jnp.where(row <= col, gram[:h, :h], gram[h:, h:])
    diag = jnp.diagonal(gram[h:, h:])
    pad = jnp.zeros((7, h), gram.dtype)
    first = jnp.concatenate([tri, diag[None, :], pad], axis=0)
    second = jnp.concatenate([gram[h:, :h], jnp.zeros((8, h), gram.dtype)], axis=0)
    return first, second


def unpack(first, second):
    h = first.shape[1]
    row = lax.broadcasted_iota(jnp.int32, (h, h), 0)
    col = lax.broadcasted_iota(jnp.int32, (h, h), 1)
    tri = first[:h]
    g11 = jnp.where(row <= col, tri, tri.T)
    g22 = jnp.where(row > col, tri, tri.T)
    g22 = jnp.where(row == col, first[h:h + 1, :], g22)
    g21 = second[:h]
    return g11, g21, g22


def all_reduce_symmetric(gram):
    stages = [("leaf", b) for b in range(lax.axis_size("leaf").bit_length() - 1)]
    stages += [("grp", b) for b in range(lax.axis_size("grp").bit_length() - 1)]
    first, second = pack(gram)
    if not stages:
        return unpack(first, second)
    axis0, bit0 = stages[0]
    low = (lax.axis_index(axis0) >> bit0) % 2 == 0
    keep = jnp.where(low, first, second)
    send = jnp.where(low, second, first)
    keep = keep + partner(send, axis0, bit0)
    for axis, bit in stages[1:]:
        keep = keep + partner(keep, axis, bit)
    other = partner(keep, axis0, bit0)
    first = jnp.where(low, keep, other)
    second = jnp.where(low, other, keep)
    return unpack(first, second)


def bounded_cos(x):
    k = jnp.round(x * (1.0 / math.pi))
    r = x - k * 3.140625
    r = r - k * 0.0009675025939941406
    r = r - k * 1.5099580252808664e-07
    r2 = r * r
    poly = -1.0 / 479001600.0 * r2 + 1.0 / 3628800.0
    poly = poly * r2 - 1.0 / 40320.0
    poly = poly * r2 + 1.0 / 720.0
    poly = poly * r2 - 1.0 / 24.0
    poly = poly * r2 + 0.5
    value = 1.0 - poly * r2
    half = k * 0.5
    return jnp.where(jnp.floor(half) == half, value, -value)


def per_device(inputs, freqs, phases, sample_weight, stored, root):
    total_rows = inputs.shape[0] * lax.axis_size("grp") * lax.axis_size("leaf")
    norm_scale = 1.0 / math.sqrt(total_rows)
    proj = jnp.dot(inputs, freqs, precision=lax.Precision.HIGHEST) + phases[None, :]
    features = jnp.sqrt(sample_weight)[:, None] * bounded_cos(proj) * norm_scale
    gram = lax.dot_general(
        features, features, (((0,), (0,)), ((), ())), precision=lax.Precision.HIGHEST
    )
    slot = lax.axis_index("grp") * lax.axis_size("leaf") + lax.axis_index("leaf")
    running = jnp.where(slot == root[0], stored[0], jnp.zeros_like(stored[0]))
    gram = gram + lax.dot_general(
        running, running, (((0,), (0,)), ((), ())), precision=lax.Precision.HIGHEST
    )
    gram = all_reduce_symmetric(gram)
    lower, inverse = cholesky_and_inverse(*gram)
    basis = lax.dot_general(
        features, inverse, (((1,), (1,)), ((), ())), precision=lax.Precision.HIGHEST
    ) * math.sqrt(total_rows)
    return (lower.T, basis)


def solution(mesh):
    return jax.shard_map(
        per_device,
        mesh=mesh,
        in_specs=(
            P(("grp", "leaf"), None),
            P(),
            P(),
            P(("grp", "leaf")),
            P(("grp", "leaf"), None, None),
            P(),
        ),
        out_specs=(P(), P(("grp", "leaf"), None)),
        check_vma=False,
    )
```

```python
import math

import jax
import jax.numpy as jnp
from jax import lax
from jax.sharding import PartitionSpec as P


def partner(array, axis, distance):
    return lax.ppermute(array, axis, [(i, i ^ 1 << distance) for i in range(lax.axis_size(axis))])


def mm(a, b):
    return jnp.dot(a, b, precision=lax.Precision.HIGHEST)


def cholesky_and_inverse(g11, g21, g22):
    h = g11.shape[0]
    eye = jnp.eye(h, dtype=g11.dtype)
    l11 = jnp.linalg.cholesky(g11)
    i11 = jax.scipy.linalg.solve_triangular(l11, eye, lower=True)
    l21 = mm(g21, i11.T)
    l22 = jnp.linalg.cholesky(g22 - mm(l21, l21.T))
    i22 = jax.scipy.linalg.solve_triangular(l22, eye, lower=True)
    i21 = -mm(i22, mm(l21, i11))
    zero = jnp.zeros_like(l11)
    lower = jnp.block([[l11, zero], [l21, l22]])
    inverse = jnp.block([[i11, zero], [i21, i22]])
    return lower, inverse


def pack(gram):
    h = gram.shape[0] // 2
    row = lax.broadcasted_iota(jnp.int32, (h, h), 0)
    col = lax.broadcasted_iota(jnp.int32, (h, h), 1)
    tri = jnp.where(row <= col, gram[:h, :h], gram[h:, h:])
    diag = jnp.sum(jnp.where(row == col, gram[h:, h:], 0.0), axis=0)
    pad = jnp.zeros((7, h), gram.dtype)
    first = jnp.concatenate([tri, diag[None, :], pad], axis=0)
    second = jnp.concatenate([gram[h:, :h], jnp.zeros((8, h), gram.dtype)], axis=0)
    return first, second


def unpack(first, second):
    h = first.shape[1]
    row = lax.broadcasted_iota(jnp.int32, (h, h), 0)
    col = lax.broadcasted_iota(jnp.int32, (h, h), 1)
    tri = first[:h]
    g11 = jnp.where(row <= col, tri, tri.T)
    g22 = jnp.where(row > col, tri, tri.T)
    g22 = jnp.where(row == col, first[h:h + 1, :], g22)
    g21 = second[:h]
    return g11, g21, g22


def flip(array, mask):
    axes = ("grp", "leaf")
    count = lax.axis_size("grp") * lax.axis_size("leaf")
    return lax.ppermute(array, axes, [(i, i ^ mask) for i in range(count)])


def all_reduce_symmetric(gram):
    bits = (lax.axis_size("grp") * lax.axis_size("leaf")).bit_length() - 1
    first, second = pack(gram)
    if bits == 0:
        return unpack(first, second)
    me = lax.axis_index("grp") * lax.axis_size("leaf") + lax.axis_index("leaf")
    low = me % 2 == 0
    keep = jnp.where(low, first, second)
    send = jnp.where(low, second, first)
    keep = keep + flip(send, 1)
    rest = list(range(1, bits))
    while rest:
        if len(rest) == 1:
            keep = keep + flip(keep, 1 << rest[0])
            rest = []
        else:
            ma, mb = 1 << rest[0], 1 << rest[1]
            near = keep + flip(keep, ma)
            far = flip(keep, mb) + flip(keep, ma | mb)
            keep = near + far
            rest = rest[2:]
    other = flip(keep, 1)
    first = jnp.where(low, keep, other)
    second = jnp.where(low, other, keep)
    return unpack(first, second)


def bounded_cos(x):
    k = jnp.round(x * (1.0 / math.pi))
    r = x - k * 3.140625
    r = r - k * 0.0009675025939941406
    r = r - k * 1.5099580252808664e-07
    r2 = r * r
    poly = -1.0 / 479001600.0 * r2 + 1.0 / 3628800.0
    poly = poly * r2 - 1.0 / 40320.0
    poly = poly * r2 + 1.0 / 720.0
    poly = poly * r2 - 1.0 / 24.0
    poly = poly * r2 + 0.5
    value = 1.0 - poly * r2
    half = k * 0.5
    return jnp.where(jnp.floor(half) == half, value, -value)


def per_device(inputs, freqs, phases, sample_weight, stored, root):
    total_rows = inputs.shape[0] * lax.axis_size("grp") * lax.axis_size("leaf")
    norm_scale = 1.0 / math.sqrt(total_rows)
    proj = jnp.dot(inputs, freqs, precision=lax.Precision.HIGHEST) + phases[None, :]
    features = jnp.sqrt(sample_weight)[:, None] * bounded_cos(proj) * norm_scale
    gram = lax.dot_general(
        features, features, (((0,), (0,)), ((), ())), precision=lax.Precision.HIGHEST
    )
    slot = lax.axis_index("grp") * lax.axis_size("leaf") + lax.axis_index("leaf")
    running = jnp.where(slot == root[0], stored[0], jnp.zeros_like(stored[0]))
    gram = gram + lax.dot_general(
        running, running, (((0,), (0,)), ((), ())), precision=lax.Precision.HIGHEST
    )
    gram = all_reduce_symmetric(gram)
    lower, inverse = cholesky_and_inverse(*gram)
    basis = lax.dot_general(
        features, inverse, (((1,), (1,)), ((), ())), precision=lax.Precision.HIGHEST
    ) * math.sqrt(total_rows)
    return (lower.T, basis)


def solution(mesh):
    return jax.shard_map(
        per_device,
        mesh=mesh,
        in_specs=(
            P(("grp", "leaf"), None),
            P(),
            P(),
            P(("grp", "leaf")),
            P(("grp", "leaf"), None, None),
            P(),
        ),
        out_specs=(P(), P(("grp", "leaf"), None)),
        check_vma=False,
    )
```

```python
import math

import jax
import jax.numpy as jnp
from jax import lax
from jax.sharding import PartitionSpec as P


def partner(array, axis, distance):
    return lax.ppermute(array, axis, [(i, i ^ 1 << distance) for i in range(lax.axis_size(axis))])


def mm(a, b):
    return jnp.dot(a, b, precision=lax.Precision.HIGHEST)


def cholesky_and_inverse(g11, g21, g22):
    h = g11.shape[0]
    eye = jnp.eye(h, dtype=g11.dtype)
    l11 = jnp.linalg.cholesky(g11)
    i11 = jax.scipy.linalg.solve_triangular(l11, eye, lower=True)
    l21 = mm(g21, i11.T)
    l22 = jnp.linalg.cholesky(g22 - mm(l21, l21.T))
    i22 = jax.scipy.linalg.solve_triangular(l22, eye, lower=True)
    i21 = -mm(i22, mm(l21, i11))
    zero = jnp.zeros_like(l11)
    lower = jnp.block([[l11, zero], [l21, l22]])
    inverse = jnp.block([[i11, zero], [i21, i22]])
    return lower, inverse


def pack(gram):
    h = gram.shape[0] // 2
    row = lax.broadcasted_iota(jnp.int32, (h, h), 0)
    col = lax.broadcasted_iota(jnp.int32, (h, h), 1)
    tri = jnp.where(row <= col, gram[:h, :h], gram[h:, h:])
    diag = jnp.sum(jnp.where(row == col, gram[h:, h:], 0.0), axis=0)
    pad = jnp.zeros((7, h), gram.dtype)
    first = jnp.concatenate([tri, diag[None, :], pad], axis=0)
    second = jnp.concatenate([gram[h:, :h], jnp.zeros((8, h), gram.dtype)], axis=0)
    return first, second


def unpack(first, second):
    h = first.shape[1]
    row = lax.broadcasted_iota(jnp.int32, (h, h), 0)
    col = lax.broadcasted_iota(jnp.int32, (h, h), 1)
    tri = first[:h]
    g11 = jnp.where(row <= col, tri, tri.T)
    g22 = jnp.where(row > col, tri, tri.T)
    g22 = jnp.where(row == col, first[h:h + 1, :], g22)
    g21 = second[:h]
    return g11, g21, g22


ROUND_BITS = 4


def flip(array, mask):
    axes = ("grp", "leaf")
    count = lax.axis_size("grp") * lax.axis_size("leaf")
    return lax.ppermute(array, axes, [(i, i ^ mask) for i in range(count)])


def all_reduce_symmetric(gram):
    bits = (lax.axis_size("grp") * lax.axis_size("leaf")).bit_length() - 1
    first, second = pack(gram)
    if bits == 0:
        return unpack(first, second)
    me = lax.axis_index("grp") * lax.axis_size("leaf") + lax.axis_index("leaf")
    low = me % 2 == 0
    keep = jnp.where(low, first, second)
    send = jnp.where(low, second, first)
    keep = keep + flip(send, 1)
    rest = list(range(1, bits))
    while rest:
        group, rest = rest[:ROUND_BITS], rest[ROUND_BITS:]
        copies = [keep]
        for m in range(1, 1 << len(group)):
            mask = sum(1 << b for k, b in enumerate(group) if m >> k & 1)
            copies.append(flip(keep, mask))
        while len(copies) > 1:
            copies = [copies[i] + copies[i + 1] for i in range(0, len(copies), 2)]
        keep = copies[0]
    other = flip(keep, 1)
    first = jnp.where(low, keep, other)
    second = jnp.where(low, other, keep)
    return unpack(first, second)


def bounded_cos(x):
    k = jnp.round(x * (1.0 / math.pi))
    r = x - k * 3.140625
    r = r - k * 0.0009675025939941406
    r = r - k * 1.5099580252808664e-07
    r2 = r * r
    poly = -1.0 / 479001600.0 * r2 + 1.0 / 3628800.0
    poly = poly * r2 - 1.0 / 40320.0
    poly = poly * r2 + 1.0 / 720.0
    poly = poly * r2 - 1.0 / 24.0
    poly = poly * r2 + 0.5
    value = 1.0 - poly * r2
    half = k * 0.5
    return jnp.where(jnp.floor(half) == half, value, -value)


def per_device(inputs, freqs, phases, sample_weight, stored, root):
    total_rows = inputs.shape[0] * lax.axis_size("grp") * lax.axis_size("leaf")
    norm_scale = 1.0 / math.sqrt(total_rows)
    proj = jnp.dot(inputs, freqs, precision=lax.Precision.HIGHEST) + phases[None, :]
    features = jnp.sqrt(sample_weight)[:, None] * bounded_cos(proj) * norm_scale
    gram = lax.dot_general(
        features, features, (((0,), (0,)), ((), ())), precision=lax.Precision.HIGHEST
    )
    slot = lax.axis_index("grp") * lax.axis_size("leaf") + lax.axis_index("leaf")
    running = jnp.where(slot == root[0], stored[0], jnp.zeros_like(stored[0]))
    gram = gram + lax.dot_general(
        running, running, (((0,), (0,)), ((), ())), precision=lax.Precision.HIGHEST
    )
    gram = all_reduce_symmetric(gram)
    lower, inverse = cholesky_and_inverse(*gram)
    basis = lax.dot_general(
        features, inverse, (((1,), (1,)), ((), ())), precision=lax.Precision.HIGHEST
    ) * math.sqrt(total_rows)
    return (lower.T, basis)


def solution(mesh):
    return jax.shard_map(
        per_device,
        mesh=mesh,
        in_specs=(
            P(("grp", "leaf"), None),
            P(),
            P(),
            P(("grp", "leaf")),
            P(("grp", "leaf"), None, None),
            P(),
        ),
        out_specs=(P(), P(("grp", "leaf"), None)),
        check_vma=False,
    )
```

```python
import math

import jax
import jax.numpy as jnp
from jax import lax
from jax.sharding import PartitionSpec as P


def partner(array, axis, distance):
    return lax.ppermute(array, axis, [(i, i ^ 1 << distance) for i in range(lax.axis_size(axis))])


def mm(a, b):
    return jnp.dot(a, b, precision=lax.Precision.HIGHEST)


def cholesky_and_inverse(g11, g21, g22):
    h = g11.shape[0]
    eye = jnp.eye(h, dtype=g11.dtype)
    l11 = lax.linalg.cholesky(g11, symmetrize_input=False)
    i11 = lax.linalg.triangular_solve(l11, eye, left_side=True, lower=True)
    l21 = mm(g21, i11.T)
    l22 = lax.linalg.cholesky(g22 - mm(l21, l21.T), symmetrize_input=False)
    i22 = lax.linalg.triangular_solve(l22, eye, left_side=True, lower=True)
    i21 = -mm(i22, mm(l21, i11))
    zero = jnp.zeros_like(l11)
    lower = jnp.block([[l11, zero], [l21, l22]])
    inverse = jnp.block([[i11, zero], [i21, i22]])
    return lower, inverse


def pack(gram):
    h = gram.shape[0] // 2
    row = lax.broadcasted_iota(jnp.int32, (h, h), 0)
    col = lax.broadcasted_iota(jnp.int32, (h, h), 1)
    tri = jnp.where(row <= col, gram[:h, :h], gram[h:, h:])
    diag = jnp.sum(jnp.where(row == col, gram[h:, h:], 0.0), axis=0)
    pad = jnp.zeros((7, h), gram.dtype)
    first = jnp.concatenate([tri, diag[None, :], pad], axis=0)
    second = jnp.concatenate([gram[h:, :h], jnp.zeros((8, h), gram.dtype)], axis=0)
    return first, second


def unpack(first, second):
    h = first.shape[1]
    row = lax.broadcasted_iota(jnp.int32, (h, h), 0)
    col = lax.broadcasted_iota(jnp.int32, (h, h), 1)
    tri = first[:h]
    g11 = jnp.where(row <= col, tri, tri.T)
    g22 = jnp.where(row > col, tri, tri.T)
    g22 = jnp.where(row == col, first[h:h + 1, :], g22)
    g21 = second[:h]
    return g11, g21, g22


def flip(array, mask):
    axes = ("grp", "leaf")
    count = lax.axis_size("grp") * lax.axis_size("leaf")
    return lax.ppermute(array, axes, [(i, i ^ mask) for i in range(count)])


def all_reduce_symmetric(gram):
    bits = (lax.axis_size("grp") * lax.axis_size("leaf")).bit_length() - 1
    first, second = pack(gram)
    if bits == 0:
        return unpack(first, second)
    me = lax.axis_index("grp") * lax.axis_size("leaf") + lax.axis_index("leaf")
    low = me % 2 == 0
    keep = jnp.where(low, first, second)
    send = jnp.where(low, second, first)
    keep = keep + flip(send, 1)
    rest = list(range(1, bits))
    while rest:
        if len(rest) == 1:
            keep = keep + flip(keep, 1 << rest[0])
            rest = []
        else:
            ma, mb = 1 << rest[0], 1 << rest[1]
            near = keep + flip(keep, ma)
            far = flip(keep, mb) + flip(keep, ma | mb)
            keep = near + far
            rest = rest[2:]
    other = flip(keep, 1)
    first = jnp.where(low, keep, other)
    second = jnp.where(low, other, keep)
    return unpack(first, second)


def bounded_cos(x):
    k = jnp.round(x * (1.0 / math.pi))
    r = x - k * 3.140625
    r = r - k * 0.0009675025939941406
    r = r - k * 1.5099580252808664e-07
    r2 = r * r
    poly = -1.0 / 479001600.0 * r2 + 1.0 / 3628800.0
    poly = poly * r2 - 1.0 / 40320.0
    poly = poly * r2 + 1.0 / 720.0
    poly = poly * r2 - 1.0 / 24.0
    poly = poly * r2 + 0.5
    value = 1.0 - poly * r2
    half = k * 0.5
    return jnp.where(jnp.floor(half) == half, value, -value)


def per_device(inputs, freqs, phases, sample_weight, stored, root):
    total_rows = inputs.shape[0] * lax.axis_size("grp") * lax.axis_size("leaf")
    norm_scale = 1.0 / math.sqrt(total_rows)
    proj = jnp.dot(inputs, freqs, precision=lax.Precision.HIGHEST) + phases[None, :]
    features = jnp.sqrt(sample_weight)[:, None] * bounded_cos(proj) * norm_scale
    gram = lax.dot_general(
        features, features, (((0,), (0,)), ((), ())), precision=lax.Precision.HIGHEST
    )
    slot = lax.axis_index("grp") * lax.axis_size("leaf") + lax.axis_index("leaf")
    running = jnp.where(slot == root[0], stored[0], jnp.zeros_like(stored[0]))
    gram = gram + lax.dot_general(
        running, running, (((0,), (0,)), ((), ())), precision=lax.Precision.HIGHEST
    )
    gram = all_reduce_symmetric(gram)
    lower, inverse = cholesky_and_inverse(*gram)
    basis = lax.dot_general(
        features, inverse, (((1,), (1,)), ((), ())), precision=lax.Precision.HIGHEST
    ) * math.sqrt(total_rows)
    return (lower.T, basis)


def solution(mesh):
    return jax.shard_map(
        per_device,
        mesh=mesh,
        in_specs=(
            P(("grp", "leaf"), None),
            P(),
            P(),
            P(("grp", "leaf")),
            P(("grp", "leaf"), None, None),
            P(),
        ),
        out_specs=(P(), P(("grp", "leaf"), None)),
        check_vma=False,
    )
```

```python
import math

import jax
import jax.numpy as jnp
from jax import lax
from jax.sharding import PartitionSpec as P


def partner(array, axis, distance):
    return lax.ppermute(array, axis, [(i, i ^ 1 << distance) for i in range(lax.axis_size(axis))])


def mm(a, b):
    return jnp.dot(a, b, precision=lax.Precision.HIGHEST)


def tmm(a, b):
    return lax.dot_general(a, b, (((0,), (0,)), ((), ())), precision=lax.Precision.HIGHEST)


def rmm(a, b):
    return lax.dot_general(a, b, (((1,), (1,)), ((), ())), precision=lax.Precision.HIGHEST)


def cholesky_and_inverse(g11, g21, g22):
    h = g11.shape[0]
    eye = jnp.eye(h, dtype=g11.dtype)
    l11 = lax.linalg.cholesky(g11, symmetrize_input=False)
    i11 = lax.linalg.triangular_solve(l11, eye, left_side=True, lower=True)
    l21 = mm(g21, i11.T)
    l22 = lax.linalg.cholesky(g22 - mm(l21, l21.T), symmetrize_input=False)
    i22 = lax.linalg.triangular_solve(l22, eye, left_side=True, lower=True)
    i21 = -mm(i22, mm(l21, i11))
    zero = jnp.zeros_like(l11)
    lower = jnp.block([[l11, zero], [l21, l22]])
    inverse = jnp.block([[i11, zero], [i21, i22]])
    return lower, inverse


def pack(g11, g12, g22):
    h = g11.shape[0]
    row = lax.broadcasted_iota(jnp.int32, (h, h), 0)
    col = lax.broadcasted_iota(jnp.int32, (h, h), 1)
    tri = jnp.where(row <= col, g11, g22)
    diag = jnp.sum(jnp.where(row == col, g22, 0.0), axis=0)
    pad = jnp.zeros((7, h), g11.dtype)
    first = jnp.concatenate([tri, diag[None, :], pad], axis=0)
    second = jnp.concatenate([g12.T, jnp.zeros((8, h), g11.dtype)], axis=0)
    return first, second


def unpack(first, second):
    h = first.shape[1]
    row = lax.broadcasted_iota(jnp.int32, (h, h), 0)
    col = lax.broadcasted_iota(jnp.int32, (h, h), 1)
    tri = first[:h]
    g11 = jnp.where(row <= col, tri, tri.T)
    g22 = jnp.where(row > col, tri, tri.T)
    g22 = jnp.where(row == col, first[h:h + 1, :], g22)
    g21 = second[:h]
    return g11, g21, g22


def flip(array, mask):
    axes = ("grp", "leaf")
    count = lax.axis_size("grp") * lax.axis_size("leaf")
    return lax.ppermute(array, axes, [(i, i ^ mask) for i in range(count)])


def all_reduce_symmetric(g11, g12, g22):
    bits = (lax.axis_size("grp") * lax.axis_size("leaf")).bit_length() - 1
    first, second = pack(g11, g12, g22)
    if bits == 0:
        return unpack(first, second)
    me = lax.axis_index("grp") * lax.axis_size("leaf") + lax.axis_index("leaf")
    low = me % 2 == 0
    keep = jnp.where(low, first, second)
    send = jnp.where(low, second, first)
    keep = keep + flip(send, 1)
    rest = list(range(1, bits))
    while rest:
        if len(rest) == 1:
            keep = keep + flip(keep, 1 << rest[0])
            rest = []
        else:
            ma, mb = 1 << rest[0], 1 << rest[1]
            near = keep + flip(keep, ma)
            far = flip(keep, mb) + flip(keep, ma | mb)
            keep = near + far
            rest = rest[2:]
    other = flip(keep, 1)
    first = jnp.where(low, keep, other)
    second = jnp.where(low, other, keep)
    return unpack(first, second)


def bounded_cos(x):
    k = jnp.round(x * (1.0 / math.pi))
    r = x - k * 3.140625
    r = r - k * 0.0009675025939941406
    r = r - k * 1.5099580252808664e-07
    r2 = r * r
    poly = -1.0 / 479001600.0 * r2 + 1.0 / 3628800.0
    poly = poly * r2 - 1.0 / 40320.0
    poly = poly * r2 + 1.0 / 720.0
    poly = poly * r2 - 1.0 / 24.0
    poly = poly * r2 + 0.5
    value = 1.0 - poly * r2
    half = k * 0.5
    return jnp.where(jnp.floor(half) == half, value, -value)


def per_device(inputs, freqs, phases, sample_weight, stored, root):
    total_rows = inputs.shape[0] * lax.axis_size("grp") * lax.axis_size("leaf")
    norm_scale = 1.0 / math.sqrt(total_rows)
    proj = jnp.dot(inputs, freqs, precision=lax.Precision.HIGHEST) + phases[None, :]
    features = jnp.sqrt(sample_weight)[:, None] * bounded_cos(proj) * norm_scale
    slot = lax.axis_index("grp") * lax.axis_size("leaf") + lax.axis_index("leaf")
    running = jnp.where(slot == root[0], stored[0], jnp.zeros_like(stored[0]))
    h = features.shape[1] // 2
    g_top = tmm(features[:, :h], features) + tmm(running[:, :h], running)
    g22 = tmm(features[:, h:], features[:, h:]) + tmm(running[:, h:], running[:, h:])
    gram = all_reduce_symmetric(g_top[:, :h], g_top[:, h:], g22)
    lower, inverse = cholesky_and_inverse(*gram)
    basis = rmm(features, inverse) * math.sqrt(total_rows)
    return (lower.T, basis)


def solution(mesh):
    return jax.shard_map(
        per_device,
        mesh=mesh,
        in_specs=(
            P(("grp", "leaf"), None),
            P(),
            P(),
            P(("grp", "leaf")),
            P(("grp", "leaf"), None, None),
            P(),
        ),
        out_specs=(P(), P(("grp", "leaf"), None)),
        check_vma=False,
    )
```

```python
import math

import jax
import jax.numpy as jnp
from jax import lax
from jax.sharding import PartitionSpec as P


def partner(array, axis, distance):
    return lax.ppermute(array, axis, [(i, i ^ 1 << distance) for i in range(lax.axis_size(axis))])


def mm(a, b):
    return jnp.dot(a, b, precision=lax.Precision.HIGHEST)


def shared_inverse(lower):
    q = lower.shape[0] // 2
    low = (lax.axis_index("grp") * lax.axis_size("leaf") + lax.axis_index("leaf")) % 2 == 0
    block = jnp.where(low, lower[:q, :q], lower[q:, q:])
    mine = lax.linalg.triangular_solve(
        block, jnp.eye(q, dtype=lower.dtype), left_side=True, lower=True
    )
    other = flip(mine, 1)
    top = jnp.where(low, mine, other)
    bottom = jnp.where(low, other, mine)
    corner = -mm(bottom, mm(lower[q:, :q], top))
    zero = jnp.zeros_like(top)
    return jnp.block([[top, zero], [corner, bottom]])


def cholesky_and_inverse(g11, g21, g22):
    l11 = lax.linalg.cholesky(g11, symmetrize_input=False)
    i11 = shared_inverse(l11)
    l21 = mm(g21, i11.T)
    l22 = lax.linalg.cholesky(g22 - mm(l21, l21.T), symmetrize_input=False)
    i22 = shared_inverse(l22)
    i21 = -mm(i22, mm(l21, i11))
    zero = jnp.zeros_like(l11)
    lower = jnp.block([[l11, zero], [l21, l22]])
    inverse = jnp.block([[i11, zero], [i21, i22]])
    return lower, inverse


def pack(gram):
    h = gram.shape[0] // 2
    row = lax.broadcasted_iota(jnp.int32, (h, h), 0)
    col = lax.broadcasted_iota(jnp.int32, (h, h), 1)
    tri = jnp.where(row <= col, gram[:h, :h], gram[h:, h:])
    diag = jnp.sum(jnp.where(row == col, gram[h:, h:], 0.0), axis=0)
    pad = jnp.zeros((7, h), gram.dtype)
    first = jnp.concatenate([tri, diag[None, :], pad], axis=0)
    second = jnp.concatenate([gram[h:, :h], jnp.zeros((8, h), gram.dtype)], axis=0)
    return first, second


def unpack(first, second):
    h = first.shape[1]
    row = lax.broadcasted_iota(jnp.int32, (h, h), 0)
    col = lax.broadcasted_iota(jnp.int32, (h, h), 1)
    tri = first[:h]
    g11 = jnp.where(row <= col, tri, tri.T)
    g22 = jnp.where(row > col, tri, tri.T)
    g22 = jnp.where(row == col, first[h:h + 1, :], g22)
    g21 = second[:h]
    return g11, g21, g22


def flip(array, mask):
    axes = ("grp", "leaf")
    count = lax.axis_size("grp") * lax.axis_size("leaf")
    return lax.ppermute(array, axes, [(i, i ^ mask) for i in range(count)])


def all_reduce_symmetric(gram):
    bits = (lax.axis_size("grp") * lax.axis_size("leaf")).bit_length() - 1
    first, second = pack(gram)
    if bits == 0:
        return unpack(first, second)
    me = lax.axis_index("grp") * lax.axis_size("leaf") + lax.axis_index("leaf")
    low = me % 2 == 0
    keep = jnp.where(low, first, second)
    send = jnp.where(low, second, first)
    keep = keep + flip(send, 1)
    rest = list(range(1, bits))
    while rest:
        if len(rest) == 1:
            keep = keep + flip(keep, 1 << rest[0])
            rest = []
        else:
            ma, mb = 1 << rest[0], 1 << rest[1]
            near = keep + flip(keep, ma)
            far = flip(keep, mb) + flip(keep, ma | mb)
            keep = near + far
            rest = rest[2:]
    other = flip(keep, 1)
    first = jnp.where(low, keep, other)
    second = jnp.where(low, other, keep)
    return unpack(first, second)


def bounded_cos(x):
    k = jnp.round(x * (1.0 / math.pi))
    r = x - k * 3.140625
    r = r - k * 0.0009675025939941406
    r = r - k * 1.5099580252808664e-07
    r2 = r * r
    poly = -1.0 / 479001600.0 * r2 + 1.0 / 3628800.0
    poly = poly * r2 - 1.0 / 40320.0
    poly = poly * r2 + 1.0 / 720.0
    poly = poly * r2 - 1.0 / 24.0
    poly = poly * r2 + 0.5
    value = 1.0 - poly * r2
    half = k * 0.5
    return jnp.where(jnp.floor(half) == half, value, -value)


def per_device(inputs, freqs, phases, sample_weight, stored, root):
    total_rows = inputs.shape[0] * lax.axis_size("grp") * lax.axis_size("leaf")
    norm_scale = 1.0 / math.sqrt(total_rows)
    proj = jnp.dot(inputs, freqs, precision=lax.Precision.HIGHEST) + phases[None, :]
    features = jnp.sqrt(sample_weight)[:, None] * bounded_cos(proj) * norm_scale
    gram = lax.dot_general(
        features, features, (((0,), (0,)), ((), ())), precision=lax.Precision.HIGHEST
    )
    slot = lax.axis_index("grp") * lax.axis_size("leaf") + lax.axis_index("leaf")
    running = jnp.where(slot == root[0], stored[0], jnp.zeros_like(stored[0]))
    gram = gram + lax.dot_general(
        running, running, (((0,), (0,)), ((), ())), precision=lax.Precision.HIGHEST
    )
    gram = all_reduce_symmetric(gram)
    lower, inverse = cholesky_and_inverse(*gram)
    basis = lax.dot_general(
        features, inverse, (((1,), (1,)), ((), ())), precision=lax.Precision.HIGHEST
    ) * math.sqrt(total_rows)
    return (lower.T, basis)


def solution(mesh):
    return jax.shard_map(
        per_device,
        mesh=mesh,
        in_specs=(
            P(("grp", "leaf"), None),
            P(),
            P(),
            P(("grp", "leaf")),
            P(("grp", "leaf"), None, None),
            P(),
        ),
        out_specs=(P(), P(("grp", "leaf"), None)),
        check_vma=False,
    )
```

```python
import math

import jax
import jax.numpy as jnp
from jax import lax
from jax.sharding import PartitionSpec as P


def partner(array, axis, distance):
    return lax.ppermute(array, axis, [(i, i ^ 1 << distance) for i in range(lax.axis_size(axis))])


def mm(a, b):
    return jnp.dot(a, b, precision=lax.Precision.HIGHEST)


def shared_inverse(lower):
    q = lower.shape[0] // 2
    low = (lax.axis_index("grp") * lax.axis_size("leaf") + lax.axis_index("leaf")) % 2 == 0
    block = jnp.where(low, lower[:q, :q], lower[q:, q:])
    mine = lax.linalg.triangular_solve(
        block, jnp.eye(q, dtype=lower.dtype), left_side=True, lower=True
    )
    other = flip(mine, 1)
    top = jnp.where(low, mine, other)
    bottom = jnp.where(low, other, mine)
    corner = -mm(bottom, mm(lower[q:, :q], top))
    zero = jnp.zeros_like(top)
    return jnp.block([[top, zero], [corner, bottom]])


def cholesky_and_inverse(g11, g21, g22):
    l11 = lax.linalg.cholesky(g11, symmetrize_input=False)
    i11 = shared_inverse(l11)
    l21 = mm(g21, i11.T)
    l22 = lax.linalg.cholesky(g22 - mm(l21, l21.T), symmetrize_input=False)
    i22 = shared_inverse(l22)
    i21 = -mm(i22, mm(l21, i11))
    zero = jnp.zeros_like(l11)
    lower = jnp.block([[l11, zero], [l21, l22]])
    inverse = jnp.block([[i11, zero], [i21, i22]])
    return lower, inverse


def pack(gram):
    h = gram.shape[0] // 2
    row = lax.broadcasted_iota(jnp.int32, (h, h), 0)
    col = lax.broadcasted_iota(jnp.int32, (h, h), 1)
    tri = jnp.where(row <= col, gram[:h, :h], gram[h:, h:])
    diag = jnp.sum(jnp.where(row == col, gram[h:, h:], 0.0), axis=0)
    pad = jnp.zeros((7, h), gram.dtype)
    first = jnp.concatenate([tri, diag[None, :], pad], axis=0)
    second = jnp.concatenate([gram[h:, :h], jnp.zeros((8, h), gram.dtype)], axis=0)
    return first, second


def unpack(first, second):
    h = first.shape[1]
    row = lax.broadcasted_iota(jnp.int32, (h, h), 0)
    col = lax.broadcasted_iota(jnp.int32, (h, h), 1)
    tri = first[:h]
    g11 = jnp.where(row <= col, tri, tri.T)
    g22 = jnp.where(row > col, tri, tri.T)
    g22 = jnp.where(row == col, first[h:h + 1, :], g22)
    g21 = second[:h]
    return g11, g21, g22


ROUND_BITS = 4


def flip(array, mask):
    axes = ("grp", "leaf")
    count = lax.axis_size("grp") * lax.axis_size("leaf")
    return lax.ppermute(array, axes, [(i, i ^ mask) for i in range(count)])


def all_reduce_symmetric(gram):
    bits = (lax.axis_size("grp") * lax.axis_size("leaf")).bit_length() - 1
    first, second = pack(gram)
    if bits == 0:
        return unpack(first, second)
    me = lax.axis_index("grp") * lax.axis_size("leaf") + lax.axis_index("leaf")
    low = me % 2 == 0
    keep = jnp.where(low, first, second)
    send = jnp.where(low, second, first)
    keep = keep + flip(send, 1)
    rest = list(range(1, bits))
    while rest:
        group, rest = rest[:ROUND_BITS], rest[ROUND_BITS:]
        copies = [keep]
        for m in range(1, 1 << len(group)):
            mask = sum(1 << b for k, b in enumerate(group) if m >> k & 1)
            copies.append(flip(keep, mask))
        while len(copies) > 1:
            copies = [copies[i] + copies[i + 1] for i in range(0, len(copies), 2)]
        keep = copies[0]
    other = flip(keep, 1)
    first = jnp.where(low, keep, other)
    second = jnp.where(low, other, keep)
    return unpack(first, second)


def bounded_cos(x):
    k = jnp.round(x * (1.0 / math.pi))
    r = x - k * 3.140625
    r = r - k * 0.0009675025939941406
    r = r - k * 1.5099580252808664e-07
    r2 = r * r
    poly = -1.0 / 479001600.0 * r2 + 1.0 / 3628800.0
    poly = poly * r2 - 1.0 / 40320.0
    poly = poly * r2 + 1.0 / 720.0
    poly = poly * r2 - 1.0 / 24.0
    poly = poly * r2 + 0.5
    value = 1.0 - poly * r2
    half = k * 0.5
    return jnp.where(jnp.floor(half) == half, value, -value)


def per_device(inputs, freqs, phases, sample_weight, stored, root):
    total_rows = inputs.shape[0] * lax.axis_size("grp") * lax.axis_size("leaf")
    norm_scale = 1.0 / math.sqrt(total_rows)
    proj = jnp.dot(inputs, freqs, precision=lax.Precision.HIGHEST) + phases[None, :]
    features = jnp.sqrt(sample_weight)[:, None] * bounded_cos(proj) * norm_scale
    gram = lax.dot_general(
        features, features, (((0,), (0,)), ((), ())), precision=lax.Precision.HIGHEST
    )
    slot = lax.axis_index("grp") * lax.axis_size("leaf") + lax.axis_index("leaf")
    running = jnp.where(slot == root[0], stored[0], jnp.zeros_like(stored[0]))
    gram = gram + lax.dot_general(
        running, running, (((0,), (0,)), ((), ())), precision=lax.Precision.HIGHEST
    )
    gram = all_reduce_symmetric(gram)
    lower, inverse = cholesky_and_inverse(*gram)
    basis = lax.dot_general(
        features, inverse, (((1,), (1,)), ((), ())), precision=lax.Precision.HIGHEST
    ) * math.sqrt(total_rows)
    return (lower.T, basis)


def solution(mesh):
    return jax.shard_map(
        per_device,
        mesh=mesh,
        in_specs=(
            P(("grp", "leaf"), None),
            P(),
            P(),
            P(("grp", "leaf")),
            P(("grp", "leaf"), None, None),
            P(),
        ),
        out_specs=(P(), P(("grp", "leaf"), None)),
        check_vma=False,
    )
```

```python
import math

import jax
import jax.numpy as jnp
from jax import lax
from jax.sharding import PartitionSpec as P


def partner(array, axis, distance):
    return lax.ppermute(array, axis, [(i, i ^ 1 << distance) for i in range(lax.axis_size(axis))])


def mm(a, b):
    return jnp.dot(a, b, precision=lax.Precision.HIGHEST)


def shared_inverse(lower):
    q = lower.shape[0] // 2
    low = (lax.axis_index("grp") * lax.axis_size("leaf") + lax.axis_index("leaf")) % 2 == 0
    block = jnp.where(low, lower[:q, :q], lower[q:, q:])
    mine = lax.linalg.triangular_solve(
        block, jnp.eye(q, dtype=lower.dtype), left_side=True, lower=True
    )
    other = flip(mine, 1)
    top = jnp.where(low, mine, other)
    bottom = jnp.where(low, other, mine)
    corner = -mm(bottom, mm(lower[q:, :q], top))
    zero = jnp.zeros_like(top)
    return jnp.block([[top, zero], [corner, bottom]])


def cholesky_and_inverse(g11, g21, g22):
    l11 = lax.linalg.cholesky(g11, symmetrize_input=False)
    i11 = shared_inverse(l11)
    l21 = mm(g21, i11.T)
    l22 = lax.linalg.cholesky(g22 - mm(l21, l21.T), symmetrize_input=False)
    i22 = shared_inverse(l22)
    i21 = -mm(i22, mm(l21, i11))
    zero = jnp.zeros_like(l11)
    lower = jnp.block([[l11, zero], [l21, l22]])
    inverse = jnp.block([[i11, zero], [i21, i22]])
    return lower, inverse


def pack(gram):
    h = gram.shape[0] // 2
    row = lax.broadcasted_iota(jnp.int32, (h, h), 0)
    col = lax.broadcasted_iota(jnp.int32, (h, h), 1)
    tri = jnp.where(row <= col, gram[:h, :h], gram[h:, h:])
    diag = jnp.sum(jnp.where(row == col, gram[h:, h:], 0.0), axis=0)
    pad = jnp.zeros((PIECE * 4 - h - 1, h), gram.dtype)
    first = jnp.concatenate([tri, diag[None, :], pad], axis=0)
    second = jnp.concatenate([gram[h:, :h], jnp.zeros((PIECE * 4 - h, h), gram.dtype)], axis=0)
    return first, second


def unpack(first, second):
    h = first.shape[1]
    row = lax.broadcasted_iota(jnp.int32, (h, h), 0)
    col = lax.broadcasted_iota(jnp.int32, (h, h), 1)
    tri = first[:h]
    g11 = jnp.where(row <= col, tri, tri.T)
    g22 = jnp.where(row > col, tri, tri.T)
    g22 = jnp.where(row == col, first[h:h + 1, :], g22)
    g21 = second[:h]
    return g11, g21, g22


PIECE = 40


def flip(array, mask):
    axes = ("grp", "leaf")
    count = lax.axis_size("grp") * lax.axis_size("leaf")
    return lax.ppermute(array, axes, [(i, i ^ mask) for i in range(count)])


def reduce_rounds(keep, rest):
    while rest:
        if len(rest) == 1:
            keep = keep + flip(keep, 1 << rest[0])
            rest = []
        else:
            ma, mb = 1 << rest[0], 1 << rest[1]
            near = keep + flip(keep, ma)
            far = flip(keep, mb) + flip(keep, ma | mb)
            keep = near + far
            rest = rest[2:]
    return keep


def all_reduce_symmetric(gram):
    bits = (lax.axis_size("grp") * lax.axis_size("leaf")).bit_length() - 1
    first, second = pack(gram)
    if bits == 0:
        return unpack(first, second)
    me = lax.axis_index("grp") * lax.axis_size("leaf") + lax.axis_index("leaf")
    low = me % 2 == 0
    keep = jnp.where(low, first, second)
    send = jnp.where(low, second, first)
    keep = keep + flip(send, 1)
    rest = list(range(1, bits))
    if len(rest) >= 2:
        b1, b2 = rest[0], rest[1]
        rest = rest[2:]
        pos = (me >> b1) % 2 + 2 * ((me >> b2) % 2)
        masks = [0, 1 << b1, 1 << b2, (1 << b1) | (1 << b2)]
        own = lax.dynamic_slice_in_dim(keep, pos * PIECE, PIECE)
        got = [own]
        for m in range(1, 4):
            part = lax.dynamic_slice_in_dim(keep, (pos ^ m) * PIECE, PIECE)
            got.append(flip(part, masks[m]))
        keep = (got[0] + got[1]) + (got[2] + got[3])
        keep = reduce_rounds(keep, rest)
        got = [keep] + [flip(keep, masks[m]) for m in range(1, 4)]
        pieces = []
        for q in range(4):
            piece = got[0]
            for m in range(1, 4):
                piece = jnp.where((pos ^ m) == q, got[m], piece)
            pieces.append(piece)
        keep = jnp.concatenate(pieces, axis=0)
    else:
        keep = reduce_rounds(keep, rest)
    other = flip(keep, 1)
    first = jnp.where(low, keep, other)
    second = jnp.where(low, other, keep)
    return unpack(first, second)


def bounded_cos(x):
    k = jnp.round(x * (1.0 / math.pi))
    r = x - k * 3.140625
    r = r - k * 0.0009675025939941406
    r = r - k * 1.5099580252808664e-07
    r2 = r * r
    poly = -1.0 / 479001600.0 * r2 + 1.0 / 3628800.0
    poly = poly * r2 - 1.0 / 40320.0
    poly = poly * r2 + 1.0 / 720.0
    poly = poly * r2 - 1.0 / 24.0
    poly = poly * r2 + 0.5
    value = 1.0 - poly * r2
    half = k * 0.5
    return jnp.where(jnp.floor(half) == half, value, -value)


def per_device(inputs, freqs, phases, sample_weight, stored, root):
    total_rows = inputs.shape[0] * lax.axis_size("grp") * lax.axis_size("leaf")
    norm_scale = 1.0 / math.sqrt(total_rows)
    proj = jnp.dot(inputs, freqs, precision=lax.Precision.HIGHEST) + phases[None, :]
    features = jnp.sqrt(sample_weight)[:, None] * bounded_cos(proj) * norm_scale
    gram = lax.dot_general(
        features, features, (((0,), (0,)), ((), ())), precision=lax.Precision.HIGHEST
    )
    slot = lax.axis_index("grp") * lax.axis_size("leaf") + lax.axis_index("leaf")
    running = jnp.where(slot == root[0], stored[0], jnp.zeros_like(stored[0]))
    gram = gram + lax.dot_general(
        running, running, (((0,), (0,)), ((), ())), precision=lax.Precision.HIGHEST
    )
    gram = all_reduce_symmetric(gram)
    lower, inverse = cholesky_and_inverse(*gram)
    basis = lax.dot_general(
        features, inverse, (((1,), (1,)), ((), ())), precision=lax.Precision.HIGHEST
    ) * math.sqrt(total_rows)
    return (lower.T, basis)


def solution(mesh):
    return jax.shard_map(
        per_device,
        mesh=mesh,
        in_specs=(
            P(("grp", "leaf"), None),
            P(),
            P(),
            P(("grp", "leaf")),
            P(("grp", "leaf"), None, None),
            P(),
        ),
        out_specs=(P(), P(("grp", "leaf"), None)),
        check_vma=False,
    )
```

```python
import math

import jax
import jax.numpy as jnp
from jax import lax
from jax.sharding import PartitionSpec as P


def partner(array, axis, distance):
    return lax.ppermute(array, axis, [(i, i ^ 1 << distance) for i in range(lax.axis_size(axis))])


def mm(a, b):
    return jnp.dot(a, b, precision=lax.Precision.HIGHEST)


def shared_inverse(lower):
    q = lower.shape[0] // 2
    low = (lax.axis_index("grp") * lax.axis_size("leaf") + lax.axis_index("leaf")) % 2 == 0
    block = jnp.where(low, lower[:q, :q], lower[q:, q:])
    mine = lax.linalg.triangular_solve(
        block, jnp.eye(q, dtype=lower.dtype), left_side=True, lower=True
    )
    other = flip(mine, 1)
    top = jnp.where(low, mine, other)
    bottom = jnp.where(low, other, mine)
    corner = -mm(bottom, mm(lower[q:, :q], top))
    zero = jnp.zeros_like(top)
    return jnp.block([[top, zero], [corner, bottom]])


def cholesky_and_inverse(g11, g21, g22):
    l11 = lax.linalg.cholesky(g11, symmetrize_input=False)
    i11 = shared_inverse(l11)
    l21 = mm(g21, i11.T)
    l22 = lax.linalg.cholesky(g22 - mm(l21, l21.T), symmetrize_input=False)
    i22 = shared_inverse(l22)
    i21 = -mm(i22, mm(l21, i11))
    zero = jnp.zeros_like(l11)
    lower = jnp.block([[l11, zero], [l21, l22]])
    inverse = jnp.block([[i11, zero], [i21, i22]])
    return lower, inverse


def pack(gram):
    h = gram.shape[0] // 2
    row = lax.broadcasted_iota(jnp.int32, (h, h), 0)
    col = lax.broadcasted_iota(jnp.int32, (h, h), 1)
    tri = jnp.where(row <= col, gram[:h, :h], gram[h:, h:])
    diag = jnp.sum(jnp.where(row == col, gram[h:, h:], 0.0), axis=0)
    pad = jnp.zeros((7, h), gram.dtype)
    first = jnp.concatenate([tri, diag[None, :], pad], axis=0)
    second = jnp.concatenate([gram[h:, :h], jnp.zeros((8, h), gram.dtype)], axis=0)
    return first, second


def unpack(first, second):
    h = first.shape[1]
    row = lax.broadcasted_iota(jnp.int32, (h, h), 0)
    col = lax.broadcasted_iota(jnp.int32, (h, h), 1)
    tri = first[:h]
    g11 = jnp.where(row <= col, tri, tri.T)
    g22 = jnp.where(row > col, tri, tri.T)
    g22 = jnp.where(row == col, first[h:h + 1, :], g22)
    g21 = second[:h]
    return g11, g21, g22


def flip(array, mask):
    axes = ("grp", "leaf")
    count = lax.axis_size("grp") * lax.axis_size("leaf")
    return lax.ppermute(array, axes, [(i, i ^ mask) for i in range(count)])


def all_reduce_symmetric(gram):
    bits = (lax.axis_size("grp") * lax.axis_size("leaf")).bit_length() - 1
    first, second = pack(gram)
    if bits == 0:
        return unpack(first, second)
    me = lax.axis_index("grp") * lax.axis_size("leaf") + lax.axis_index("leaf")
    low = me % 2 == 0
    keep = jnp.where(low, first, second)
    send = jnp.where(low, second, first)
    keep = keep + flip(send, 1)
    rest = list(range(1, bits))
    while rest:
        if len(rest) == 1:
            keep = keep + flip(keep, 1 << rest[0])
            rest = []
        else:
            ma, mb = 1 << rest[0], 1 << rest[1]
            near = keep + flip(keep, ma)
            far = flip(keep, mb) + flip(keep, ma | mb)
            keep = near + far
            rest = rest[2:]
    other = flip(keep, 1)
    first = jnp.where(low, keep, other)
    second = jnp.where(low, other, keep)
    return unpack(first, second)


def bounded_cos(x):
    k = jnp.round(x * (1.0 / math.pi))
    r = x - k * 3.140625
    r = r - k * 0.0009675025939941406
    r = r - k * 1.5099580252808664e-07
    r2 = r * r
    poly = -1.0 / 479001600.0 * r2 + 1.0 / 3628800.0
    poly = poly * r2 - 1.0 / 40320.0
    poly = poly * r2 + 1.0 / 720.0
    poly = poly * r2 - 1.0 / 24.0
    poly = poly * r2 + 0.5
    value = 1.0 - poly * r2
    half = k * 0.5
    return jnp.where(jnp.floor(half) == half, value, -value)


def split_gram(f):
    def tdot(a, b):
        return lax.dot_general(a, b, (((0,), (0,)), ((), ())), preferred_element_type=jnp.float32)

    high = f.astype(jnp.bfloat16)
    rest = f - high.astype(jnp.float32)
    mid = rest.astype(jnp.bfloat16)
    low = (rest - mid.astype(jnp.float32)).astype(jnp.bfloat16)
    cross = tdot(high, mid) + tdot(high, low)
    return tdot(high, high) + (cross + cross.T) + tdot(mid, mid)


def per_device(inputs, freqs, phases, sample_weight, stored, root):
    total_rows = inputs.shape[0] * lax.axis_size("grp") * lax.axis_size("leaf")
    norm_scale = 1.0 / math.sqrt(total_rows)
    proj = jnp.dot(inputs, freqs, precision=lax.Precision.HIGHEST) + phases[None, :]
    features = jnp.sqrt(sample_weight)[:, None] * bounded_cos(proj) * norm_scale
    gram = split_gram(features)
    slot = lax.axis_index("grp") * lax.axis_size("leaf") + lax.axis_index("leaf")
    running = jnp.where(slot == root[0], stored[0], jnp.zeros_like(stored[0]))
    gram = gram + lax.dot_general(
        running, running, (((0,), (0,)), ((), ())), precision=lax.Precision.HIGHEST
    )
    gram = all_reduce_symmetric(gram)
    lower, inverse = cholesky_and_inverse(*gram)
    basis = lax.dot_general(
        features, inverse, (((1,), (1,)), ((), ())), precision=lax.Precision.HIGHEST
    ) * math.sqrt(total_rows)
    return (lower.T, basis)


def solution(mesh):
    return jax.shard_map(
        per_device,
        mesh=mesh,
        in_specs=(
            P(("grp", "leaf"), None),
            P(),
            P(),
            P(("grp", "leaf")),
            P(("grp", "leaf"), None, None),
            P(),
        ),
        out_specs=(P(), P(("grp", "leaf"), None)),
        check_vma=False,
    )
```

```python
import math

import jax
import jax.numpy as jnp
from jax import lax
from jax.sharding import PartitionSpec as P


def partner(array, axis, distance):
    return lax.ppermute(array, axis, [(i, i ^ 1 << distance) for i in range(lax.axis_size(axis))])


def mm(a, b):
    return jnp.dot(a, b, precision=lax.Precision.HIGHEST)


def shared_inverse(lower):
    q = lower.shape[0] // 2
    low = (lax.axis_index("grp") * lax.axis_size("leaf") + lax.axis_index("leaf")) % 2 == 0
    block = jnp.where(low, lower[:q, :q], lower[q:, q:])
    mine = lax.linalg.triangular_solve(
        block, jnp.eye(q, dtype=lower.dtype), left_side=True, lower=True
    )
    other = flip(mine, 1)
    top = jnp.where(low, mine, other)
    bottom = jnp.where(low, other, mine)
    corner = -mm(bottom, mm(lower[q:, :q], top))
    zero = jnp.zeros_like(top)
    return jnp.block([[top, zero], [corner, bottom]])


def cholesky_and_inverse(g11, g21, g22):
    l11 = lax.linalg.cholesky(g11, symmetrize_input=False)
    i11 = shared_inverse(l11)
    l21 = mm(g21, i11.T)
    l22 = lax.linalg.cholesky(g22 - mm(l21, l21.T), symmetrize_input=False)
    i22 = shared_inverse(l22)
    i21 = -mm(i22, mm(l21, i11))
    zero = jnp.zeros_like(l11)
    lower = jnp.block([[l11, zero], [l21, l22]])
    inverse = jnp.block([[i11, zero], [i21, i22]])
    return lower, inverse


def pack(gram):
    h = gram.shape[0] // 2
    row = lax.broadcasted_iota(jnp.int32, (h, h), 0)
    col = lax.broadcasted_iota(jnp.int32, (h, h), 1)
    tri = jnp.where(row <= col, gram[:h, :h], gram[h:, h:])
    diag = jnp.sum(jnp.where(row == col, gram[h:, h:], 0.0), axis=0)
    pad = jnp.zeros((7, h), gram.dtype)
    first = jnp.concatenate([tri, diag[None, :], pad], axis=0)
    second = jnp.concatenate([gram[h:, :h], jnp.zeros((8, h), gram.dtype)], axis=0)
    return first, second


def unpack(first, second):
    h = first.shape[1]
    row = lax.broadcasted_iota(jnp.int32, (h, h), 0)
    col = lax.broadcasted_iota(jnp.int32, (h, h), 1)
    tri = first[:h]
    g11 = jnp.where(row <= col, tri, tri.T)
    g22 = jnp.where(row > col, tri, tri.T)
    g22 = jnp.where(row == col, first[h:h + 1, :], g22)
    g21 = second[:h]
    return g11, g21, g22


def flip(array, mask):
    axes = ("grp", "leaf")
    count = lax.axis_size("grp") * lax.axis_size("leaf")
    return lax.ppermute(array, axes, [(i, i ^ mask) for i in range(count)])


def all_reduce_symmetric(gram):
    bits = (lax.axis_size("grp") * lax.axis_size("leaf")).bit_length() - 1
    first, second = pack(gram)
    if bits == 0:
        return unpack(first, second)
    me = lax.axis_index("grp") * lax.axis_size("leaf") + lax.axis_index("leaf")
    low = me % 2 == 0
    keep = jnp.where(low, first, second)
    send = jnp.where(low, second, first)
    keep = keep + flip(send, 1)
    rest = list(range(1, bits))
    while rest:
        if len(rest) == 1:
            keep = keep + flip(keep, 1 << rest[0])
            rest = []
        else:
            ma, mb = 1 << rest[0], 1 << rest[1]
            near = keep + flip(keep, ma)
            far = flip(keep, mb) + flip(keep, ma | mb)
            keep = near + far
            rest = rest[2:]
    other = flip(keep, 1)
    first = jnp.where(low, keep, other)
    second = jnp.where(low, other, keep)
    return unpack(first, second)


def bounded_cos(x):
    k = jnp.round(x * (1.0 / math.pi))
    r = x - k * 3.140625
    r = r - k * 0.0009675025939941406
    r = r - k * 1.5099580252808664e-07
    r2 = r * r
    poly = -1.0 / 479001600.0 * r2 + 1.0 / 3628800.0
    poly = poly * r2 - 1.0 / 40320.0
    poly = poly * r2 + 1.0 / 720.0
    poly = poly * r2 - 1.0 / 24.0
    poly = poly * r2 + 0.5
    value = 1.0 - poly * r2
    half = k * 0.5
    return jnp.where(jnp.floor(half) == half, value, -value)


def split_gram(f):
    def tdot(a, b):
        return lax.dot_general(a, b, (((0,), (0,)), ((), ())), preferred_element_type=jnp.float32)

    top = lax.reduce_precision(f, exponent_bits=8, mantissa_bits=7)
    rest = f - top
    middle = lax.reduce_precision(rest, exponent_bits=8, mantissa_bits=7)
    high = top.astype(jnp.bfloat16)
    mid = middle.astype(jnp.bfloat16)
    low = (rest - middle).astype(jnp.bfloat16)
    cross = tdot(high, mid) + tdot(high, low)
    return tdot(high, high) + (cross + cross.T) + tdot(mid, mid)


def per_device(inputs, freqs, phases, sample_weight, stored, root):
    total_rows = inputs.shape[0] * lax.axis_size("grp") * lax.axis_size("leaf")
    norm_scale = 1.0 / math.sqrt(total_rows)
    proj = jnp.dot(inputs, freqs, precision=lax.Precision.HIGHEST) + phases[None, :]
    features = jnp.sqrt(sample_weight)[:, None] * bounded_cos(proj) * norm_scale
    gram = split_gram(features)
    slot = lax.axis_index("grp") * lax.axis_size("leaf") + lax.axis_index("leaf")
    running = jnp.where(slot == root[0], stored[0], jnp.zeros_like(stored[0]))
    gram = gram + lax.dot_general(
        running, running, (((0,), (0,)), ((), ())), precision=lax.Precision.HIGHEST
    )
    gram = all_reduce_symmetric(gram)
    lower, inverse = cholesky_and_inverse(*gram)
    basis = lax.dot_general(
        features, inverse, (((1,), (1,)), ((), ())), precision=lax.Precision.HIGHEST
    ) * math.sqrt(total_rows)
    return (lower.T, basis)


def solution(mesh):
    return jax.shard_map(
        per_device,
        mesh=mesh,
        in_specs=(
            P(("grp", "leaf"), None),
            P(),
            P(),
            P(("grp", "leaf")),
            P(("grp", "leaf"), None, None),
            P(),
        ),
        out_specs=(P(), P(("grp", "leaf"), None)),
        check_vma=False,
    )
```

```python
import math

import jax
import jax.numpy as jnp
from jax import lax
from jax.sharding import PartitionSpec as P


def partner(array, axis, distance):
    return lax.ppermute(array, axis, [(i, i ^ 1 << distance) for i in range(lax.axis_size(axis))])


def mm(a, b):
    return jnp.dot(a, b, precision=lax.Precision.HIGHEST)


def shared_inverse(lower):
    q = lower.shape[0] // 2
    low = (lax.axis_index("grp") * lax.axis_size("leaf") + lax.axis_index("leaf")) % 2 == 0
    block = jnp.where(low, lower[:q, :q], lower[q:, q:])
    mine = lax.linalg.triangular_solve(
        block, jnp.eye(q, dtype=lower.dtype), left_side=True, lower=True
    )
    other = flip(mine, 1)
    top = jnp.where(low, mine, other)
    bottom = jnp.where(low, other, mine)
    corner = -mm(bottom, mm(lower[q:, :q], top))
    zero = jnp.zeros_like(top)
    return jnp.block([[top, zero], [corner, bottom]])


def cholesky_and_inverse(g11, g21, g22):
    l11 = lax.linalg.cholesky(g11, symmetrize_input=False)
    i11 = shared_inverse(l11)
    l21 = mm(g21, i11.T)
    l22 = lax.linalg.cholesky(g22 - mm(l21, l21.T), symmetrize_input=False)
    i22 = shared_inverse(l22)
    i21 = -mm(i22, mm(l21, i11))
    zero = jnp.zeros_like(l11)
    lower = jnp.block([[l11, zero], [l21, l22]])
    inverse = jnp.block([[i11, zero], [i21, i22]])
    return lower, inverse


def pack(gram):
    h = gram.shape[0] // 2
    row = lax.broadcasted_iota(jnp.int32, (h, h), 0)
    col = lax.broadcasted_iota(jnp.int32, (h, h), 1)
    tri = jnp.where(row <= col, gram[:h, :h], gram[h:, h:])
    diag = jnp.sum(jnp.where(row == col, gram[h:, h:], 0.0), axis=0)
    pad = jnp.zeros((7, h), gram.dtype)
    first = jnp.concatenate([tri, diag[None, :], pad], axis=0)
    second = jnp.concatenate([gram[h:, :h], jnp.zeros((8, h), gram.dtype)], axis=0)
    return first, second


def unpack(first, second):
    h = first.shape[1]
    row = lax.broadcasted_iota(jnp.int32, (h, h), 0)
    col = lax.broadcasted_iota(jnp.int32, (h, h), 1)
    tri = first[:h]
    g11 = jnp.where(row <= col, tri, tri.T)
    g22 = jnp.where(row > col, tri, tri.T)
    g22 = jnp.where(row == col, first[h:h + 1, :], g22)
    g21 = second[:h]
    return g11, g21, g22


def flip(array, mask):
    axes = ("grp", "leaf")
    count = lax.axis_size("grp") * lax.axis_size("leaf")
    return lax.ppermute(array, axes, [(i, i ^ mask) for i in range(count)])


def all_reduce_symmetric(gram):
    bits = (lax.axis_size("grp") * lax.axis_size("leaf")).bit_length() - 1
    first, second = pack(gram)
    if bits == 0:
        return unpack(first, second)
    me = lax.axis_index("grp") * lax.axis_size("leaf") + lax.axis_index("leaf")
    low = me % 2 == 0
    keep = jnp.where(low, first, second)
    send = jnp.where(low, second, first)
    keep = keep + flip(send, 1)
    rest = list(range(1, bits))
    rest = rest[2:4] + rest[:2] + rest[4:]
    while rest:
        if len(rest) == 1:
            keep = keep + flip(keep, 1 << rest[0])
            rest = []
        else:
            ma, mb = 1 << rest[0], 1 << rest[1]
            near = keep + flip(keep, ma)
            far = flip(keep, mb) + flip(keep, ma | mb)
            keep = near + far
            rest = rest[2:]
    other = flip(keep, 1)
    first = jnp.where(low, keep, other)
    second = jnp.where(low, other, keep)
    return unpack(first, second)


def bounded_cos(x):
    k = jnp.round(x * (1.0 / math.pi))
    r = x - k * 3.140625
    r = r - k * 0.0009675025939941406
    r = r - k * 1.5099580252808664e-07
    r2 = r * r
    poly = -1.0 / 479001600.0 * r2 + 1.0 / 3628800.0
    poly = poly * r2 - 1.0 / 40320.0
    poly = poly * r2 + 1.0 / 720.0
    poly = poly * r2 - 1.0 / 24.0
    poly = poly * r2 + 0.5
    value = 1.0 - poly * r2
    half = k * 0.5
    return jnp.where(jnp.floor(half) == half, value, -value)


def split_gram(f):
    def tdot(a, b):
        return lax.dot_general(a, b, (((0,), (0,)), ((), ())), preferred_element_type=jnp.float32)

    top = lax.reduce_precision(f, exponent_bits=8, mantissa_bits=7)
    rest = f - top
    middle = lax.reduce_precision(rest, exponent_bits=8, mantissa_bits=7)
    high = top.astype(jnp.bfloat16)
    mid = middle.astype(jnp.bfloat16)
    low = (rest - middle).astype(jnp.bfloat16)
    cross = tdot(high, mid) + tdot(high, low)
    return tdot(high, high) + (cross + cross.T) + tdot(mid, mid)


def per_device(inputs, freqs, phases, sample_weight, stored, root):
    total_rows = inputs.shape[0] * lax.axis_size("grp") * lax.axis_size("leaf")
    norm_scale = 1.0 / math.sqrt(total_rows)
    proj = jnp.dot(inputs, freqs, precision=lax.Precision.HIGHEST) + phases[None, :]
    features = jnp.sqrt(sample_weight)[:, None] * bounded_cos(proj) * norm_scale
    gram = split_gram(features)
    slot = lax.axis_index("grp") * lax.axis_size("leaf") + lax.axis_index("leaf")
    running = jnp.where(slot == root[0], stored[0], jnp.zeros_like(stored[0]))
    gram = gram + lax.dot_general(
        running, running, (((0,), (0,)), ((), ())), precision=lax.Precision.HIGHEST
    )
    gram = all_reduce_symmetric(gram)
    lower, inverse = cholesky_and_inverse(*gram)
    basis = lax.dot_general(
        features, inverse, (((1,), (1,)), ((), ())), precision=lax.Precision.HIGHEST
    ) * math.sqrt(total_rows)
    return (lower.T, basis)


def solution(mesh):
    return jax.shard_map(
        per_device,
        mesh=mesh,
        in_specs=(
            P(("grp", "leaf"), None),
            P(),
            P(),
            P(("grp", "leaf")),
            P(("grp", "leaf"), None, None),
            P(),
        ),
        out_specs=(P(), P(("grp", "leaf"), None)),
        check_vma=False,
    )
```

```python
import math

import jax
import jax.numpy as jnp
from jax import lax
from jax.sharding import PartitionSpec as P


def partner(array, axis, distance):
    return lax.ppermute(array, axis, [(i, i ^ 1 << distance) for i in range(lax.axis_size(axis))])


def mm(a, b):
    return jnp.dot(a, b, precision=lax.Precision.HIGHEST)


def shared_inverse(lower):
    q = lower.shape[0] // 2
    low = (lax.axis_index("grp") * lax.axis_size("leaf") + lax.axis_index("leaf")) % 2 == 0
    block = jnp.where(low, lower[:q, :q], lower[q:, q:])
    mine = lax.linalg.triangular_solve(
        block, jnp.eye(q, dtype=lower.dtype), left_side=True, lower=True
    )
    other = flip(mine, 1)
    top = jnp.where(low, mine, other)
    bottom = jnp.where(low, other, mine)
    corner = -mm(bottom, mm(lower[q:, :q], top))
    zero = jnp.zeros_like(top)
    return jnp.block([[top, zero], [corner, bottom]])


def cholesky_and_inverse(g11, g21, g22):
    l11 = lax.linalg.cholesky(g11, symmetrize_input=False)
    i11 = shared_inverse(l11)
    l21 = mm(g21, i11.T)
    l22 = lax.linalg.cholesky(g22 - mm(l21, l21.T), symmetrize_input=False)
    i22 = shared_inverse(l22)
    i21 = -mm(i22, mm(l21, i11))
    zero = jnp.zeros_like(l11)
    lower = jnp.block([[l11, zero], [l21, l22]])
    inverse = jnp.block([[i11, zero], [i21, i22]])
    return lower, inverse


def pack(gram):
    h = gram.shape[0] // 2
    row = lax.broadcasted_iota(jnp.int32, (h, h), 0)
    col = lax.broadcasted_iota(jnp.int32, (h, h), 1)
    tri = jnp.where(row <= col, gram[:h, :h], gram[h:, h:])
    diag = jnp.sum(jnp.where(row == col, gram[h:, h:], 0.0), axis=0)
    pad = jnp.zeros((7, h), gram.dtype)
    first = jnp.concatenate([tri, diag[None, :], pad], axis=0)
    second = jnp.concatenate([gram[h:, :h], jnp.zeros((8, h), gram.dtype)], axis=0)
    return first, second


def unpack(first, second):
    h = first.shape[1]
    row = lax.broadcasted_iota(jnp.int32, (h, h), 0)
    col = lax.broadcasted_iota(jnp.int32, (h, h), 1)
    tri = first[:h]
    g11 = jnp.where(row <= col, tri, tri.T)
    g22 = jnp.where(row > col, tri, tri.T)
    g22 = jnp.where(row == col, first[h:h + 1, :], g22)
    g21 = second[:h]
    return g11, g21, g22


def flip(array, mask):
    axes = ("grp", "leaf")
    count = lax.axis_size("grp") * lax.axis_size("leaf")
    return lax.ppermute(array, axes, [(i, i ^ mask) for i in range(count)])


def all_reduce_symmetric(gram):
    bits = (lax.axis_size("grp") * lax.axis_size("leaf")).bit_length() - 1
    first, second = pack(gram)
    if bits == 0:
        return unpack(first, second)
    h = first.shape[0]
    keep = jnp.concatenate([first, second], axis=0)
    keep = keep + flip(keep, 1)
    rest = list(range(1, bits))
    while rest:
        if len(rest) == 1:
            keep = keep + flip(keep, 1 << rest[0])
            rest = []
        else:
            ma, mb = 1 << rest[0], 1 << rest[1]
            near = keep + flip(keep, ma)
            far = flip(keep, mb) + flip(keep, ma | mb)
            keep = near + far
            rest = rest[2:]
    first, second = keep[:h], keep[h:]
    return unpack(first, second)


def bounded_cos(x):
    k = jnp.round(x * (1.0 / math.pi))
    r = x - k * 3.140625
    r = r - k * 0.0009675025939941406
    r = r - k * 1.5099580252808664e-07
    r2 = r * r
    poly = -1.0 / 479001600.0 * r2 + 1.0 / 3628800.0
    poly = poly * r2 - 1.0 / 40320.0
    poly = poly * r2 + 1.0 / 720.0
    poly = poly * r2 - 1.0 / 24.0
    poly = poly * r2 + 0.5
    value = 1.0 - poly * r2
    half = k * 0.5
    return jnp.where(jnp.floor(half) == half, value, -value)


def split_gram(f):
    def tdot(a, b):
        return lax.dot_general(a, b, (((0,), (0,)), ((), ())), preferred_element_type=jnp.float32)

    top = lax.reduce_precision(f, exponent_bits=8, mantissa_bits=7)
    rest = f - top
    middle = lax.reduce_precision(rest, exponent_bits=8, mantissa_bits=7)
    high = top.astype(jnp.bfloat16)
    mid = middle.astype(jnp.bfloat16)
    low = (rest - middle).astype(jnp.bfloat16)
    cross = tdot(high, mid) + tdot(high, low)
    return tdot(high, high) + (cross + cross.T) + tdot(mid, mid)


def per_device(inputs, freqs, phases, sample_weight, stored, root):
    total_rows = inputs.shape[0] * lax.axis_size("grp") * lax.axis_size("leaf")
    norm_scale = 1.0 / math.sqrt(total_rows)
    proj = jnp.dot(inputs, freqs, precision=lax.Precision.HIGHEST) + phases[None, :]
    features = jnp.sqrt(sample_weight)[:, None] * bounded_cos(proj) * norm_scale
    gram = split_gram(features)
    slot = lax.axis_index("grp") * lax.axis_size("leaf") + lax.axis_index("leaf")
    running = jnp.where(slot == root[0], stored[0], jnp.zeros_like(stored[0]))
    gram = gram + lax.dot_general(
        running, running, (((0,), (0,)), ((), ())), precision=lax.Precision.HIGHEST
    )
    gram = all_reduce_symmetric(gram)
    lower, inverse = cholesky_and_inverse(*gram)
    basis = lax.dot_general(
        features, inverse, (((1,), (1,)), ((), ())), precision=lax.Precision.HIGHEST
    ) * math.sqrt(total_rows)
    return (lower.T, basis)


def solution(mesh):
    return jax.shard_map(
        per_device,
        mesh=mesh,
        in_specs=(
            P(("grp", "leaf"), None),
            P(),
            P(),
            P(("grp", "leaf")),
            P(("grp", "leaf"), None, None),
            P(),
        ),
        out_specs=(P(), P(("grp", "leaf"), None)),
        check_vma=False,
    )
```

```python
import math

import jax
import jax.numpy as jnp
from jax import lax
from jax.sharding import PartitionSpec as P


def partner(array, axis, distance):
    return lax.ppermute(array, axis, [(i, i ^ 1 << distance) for i in range(lax.axis_size(axis))])


def mm(a, b):
    return jnp.dot(a, b, precision=lax.Precision.HIGHEST)


def shared_inverse(lower):
    q = lower.shape[0] // 2
    low = (lax.axis_index("grp") * lax.axis_size("leaf") + lax.axis_index("leaf")) % 2 == 0
    block = jnp.where(low, lower[:q, :q], lower[q:, q:])
    mine = lax.linalg.triangular_solve(
        block, jnp.eye(q, dtype=lower.dtype), left_side=True, lower=True
    )
    other = flip(mine, 1)
    top = jnp.where(low, mine, other)
    bottom = jnp.where(low, other, mine)
    corner = -mm(bottom, mm(lower[q:, :q], top))
    zero = jnp.zeros_like(top)
    return jnp.block([[top, zero], [corner, bottom]])


def cholesky_and_inverse(g11, g21, g22):
    l11 = lax.linalg.cholesky(g11, symmetrize_input=False)
    i11 = shared_inverse(l11)
    l21 = mm(g21, i11.T)
    l22 = lax.linalg.cholesky(g22 - mm(l21, l21.T), symmetrize_input=False)
    i22 = shared_inverse(l22)
    i21 = -mm(i22, mm(l21, i11))
    zero = jnp.zeros_like(l11)
    lower = jnp.block([[l11, zero], [l21, l22]])
    inverse = jnp.block([[i11, zero], [i21, i22]])
    return lower, inverse


def pack(gram):
    h = gram.shape[0] // 2
    row = lax.broadcasted_iota(jnp.int32, (h, h), 0)
    col = lax.broadcasted_iota(jnp.int32, (h, h), 1)
    tri = jnp.where(row <= col, gram[:h, :h], gram[h:, h:])
    diag = jnp.sum(jnp.where(row == col, gram[h:, h:], 0.0), axis=0)
    pad = jnp.zeros((7, h), gram.dtype)
    first = jnp.concatenate([tri, diag[None, :], pad], axis=0)
    second = jnp.concatenate([gram[h:, :h], jnp.zeros((8, h), gram.dtype)], axis=0)
    return first, second


def unpack(first, second):
    h = first.shape[1]
    row = lax.broadcasted_iota(jnp.int32, (h, h), 0)
    col = lax.broadcasted_iota(jnp.int32, (h, h), 1)
    tri = first[:h]
    g11 = jnp.where(row <= col, tri, tri.T)
    g22 = jnp.where(row > col, tri, tri.T)
    g22 = jnp.where(row == col, first[h:h + 1, :], g22)
    g21 = second[:h]
    return g11, g21, g22


def flip(array, mask):
    axes = ("grp", "leaf")
    count = lax.axis_size("grp") * lax.axis_size("leaf")
    return lax.ppermute(array, axes, [(i, i ^ mask) for i in range(count)])


def all_reduce_symmetric(gram):
    bits = (lax.axis_size("grp") * lax.axis_size("leaf")).bit_length() - 1
    first, second = pack(gram)
    if bits == 0:
        return unpack(first, second)
    me = lax.axis_index("grp") * lax.axis_size("leaf") + lax.axis_index("leaf")
    low = me % 2 == 0
    keep = jnp.where(low, first, second)
    send = jnp.where(low, second, first)
    keep = keep + flip(send, 1)
    rest = list(range(1, bits))
    while rest:
        if len(rest) == 1:
            keep = keep + flip(keep, 1 << rest[0])
            rest = []
        else:
            ma, mb = 1 << rest[0], 1 << rest[1]
            near = keep + flip(keep, ma)
            far = flip(keep, mb) + flip(keep, ma | mb)
            keep = near + far
            rest = rest[2:]
    other = flip(keep, 1)
    first = jnp.where(low, keep, other)
    second = jnp.where(low, other, keep)
    return unpack(first, second)


def bounded_cos(x):
    k = jnp.round(x * (1.0 / math.pi))
    r = x - k * 3.140625
    r = r - k * 0.0009675025939941406
    r = r - k * 1.5099580252808664e-07
    r2 = r * r
    poly = -1.0 / 479001600.0 * r2 + 1.0 / 3628800.0
    poly = poly * r2 - 1.0 / 40320.0
    poly = poly * r2 + 1.0 / 720.0
    poly = poly * r2 - 1.0 / 24.0
    poly = poly * r2 + 0.5
    value = 1.0 - poly * r2
    half = k * 0.5
    return jnp.where(jnp.floor(half) == half, value, -value)


def split_gram(f):
    def tdot(a, b):
        return lax.dot_general(a, b, (((0,), (0,)), ((), ())), preferred_element_type=jnp.float32)

    top = lax.reduce_precision(f, exponent_bits=8, mantissa_bits=7)
    rest = f - top
    middle = lax.reduce_precision(rest, exponent_bits=8, mantissa_bits=7)
    high = top.astype(jnp.bfloat16)
    mid = middle.astype(jnp.bfloat16)
    low = (rest - middle).astype(jnp.bfloat16)
    cross = tdot(high, mid) + tdot(high, low)
    return tdot(high, high) + (cross + cross.T) + tdot(mid, mid)


def per_device(inputs, freqs, phases, sample_weight, stored, root):
    total_rows = inputs.shape[0] * lax.axis_size("grp") * lax.axis_size("leaf")
    norm_scale = 1.0 / math.sqrt(total_rows)
    proj = jnp.dot(inputs, freqs, precision=lax.Precision.HIGHEST) + phases[None, :]
    features = jnp.sqrt(sample_weight)[:, None] * bounded_cos(proj) * norm_scale
    slot = lax.axis_index("grp") * lax.axis_size("leaf") + lax.axis_index("leaf")
    running = jnp.where(slot == root[0], stored[0], jnp.zeros_like(stored[0]))
    gram = split_gram(jnp.concatenate([features, running], axis=0))
    gram = all_reduce_symmetric(gram)
    lower, inverse = cholesky_and_inverse(*gram)
    basis = lax.dot_general(
        features, inverse, (((1,), (1,)), ((), ())), precision=lax.Precision.HIGHEST
    ) * math.sqrt(total_rows)
    return (lower.T, basis)


def solution(mesh):
    return jax.shard_map(
        per_device,
        mesh=mesh,
        in_specs=(
            P(("grp", "leaf"), None),
            P(),
            P(),
            P(("grp", "leaf")),
            P(("grp", "leaf"), None, None),
            P(),
        ),
        out_specs=(P(), P(("grp", "leaf"), None)),
        check_vma=False,
    )
```

```python
import math

import jax
import jax.numpy as jnp
from jax import lax
from jax.sharding import PartitionSpec as P


def partner(array, axis, distance):
    return lax.ppermute(array, axis, [(i, i ^ 1 << distance) for i in range(lax.axis_size(axis))])


def mm(a, b):
    return jnp.dot(a, b, precision=lax.Precision.HIGHEST)


def shared_inverse(lower):
    q = lower.shape[0] // 2
    low = (lax.axis_index("grp") * lax.axis_size("leaf") + lax.axis_index("leaf")) % 2 == 0
    block = jnp.where(low, lower[:q, :q], lower[q:, q:])
    mine = lax.linalg.triangular_solve(
        block, jnp.eye(q, dtype=lower.dtype), left_side=True, lower=True
    )
    other = flip(mine, 1)
    top = jnp.where(low, mine, other)
    bottom = jnp.where(low, other, mine)
    corner = -mm(bottom, mm(lower[q:, :q], top))
    zero = jnp.zeros_like(top)
    return jnp.block([[top, zero], [corner, bottom]])


def cholesky_and_inverse(g11, g21, g22):
    l11 = lax.linalg.cholesky(g11, symmetrize_input=False)
    i11 = shared_inverse(l11)
    l21 = mm(g21, i11.T)
    l22 = lax.linalg.cholesky(g22 - mm(l21, l21.T), symmetrize_input=False)
    i22 = shared_inverse(l22)
    i21 = -mm(i22, mm(l21, i11))
    zero = jnp.zeros_like(l11)
    lower = jnp.block([[l11, zero], [l21, l22]])
    inverse = jnp.block([[i11, zero], [i21, i22]])
    return lower, inverse


def pack(gram):
    h = gram.shape[0] // 2
    row = lax.broadcasted_iota(jnp.int32, (h, h), 0)
    col = lax.broadcasted_iota(jnp.int32, (h, h), 1)
    tri = jnp.where(row <= col, gram[:h, :h], gram[h:, h:])
    diag = jnp.sum(jnp.where(row == col, gram[h:, h:], 0.0), axis=0)
    pad = jnp.zeros((7, h), gram.dtype)
    first = jnp.concatenate([tri, diag[None, :], pad], axis=0)
    second = jnp.concatenate([gram[h:, :h], jnp.zeros((8, h), gram.dtype)], axis=0)
    return first, second


def unpack(first, second):
    h = first.shape[1]
    row = lax.broadcasted_iota(jnp.int32, (h, h), 0)
    col = lax.broadcasted_iota(jnp.int32, (h, h), 1)
    tri = first[:h]
    g11 = jnp.where(row <= col, tri, tri.T)
    g22 = jnp.where(row > col, tri, tri.T)
    g22 = jnp.where(row == col, first[h:h + 1, :], g22)
    g21 = second[:h]
    return g11, g21, g22


def flip(array, mask):
    axes = ("grp", "leaf")
    count = lax.axis_size("grp") * lax.axis_size("leaf")
    return lax.ppermute(array, axes, [(i, i ^ mask) for i in range(count)])


def all_reduce_symmetric(gram):
    bits = (lax.axis_size("grp") * lax.axis_size("leaf")).bit_length() - 1
    first, second = pack(gram)
    if bits == 0:
        return unpack(first, second)
    me = lax.axis_index("grp") * lax.axis_size("leaf") + lax.axis_index("leaf")
    low = me % 2 == 0
    keep = jnp.where(low, first, second)
    send = jnp.where(low, second, first)
    keep = keep + flip(send, 1)
    rest = list(range(1, bits))
    while rest:
        if len(rest) == 1:
            keep = keep + flip(keep, 1 << rest[0])
            rest = []
        else:
            ma, mb = 1 << rest[0], 1 << rest[1]
            near = keep + flip(keep, ma)
            far = flip(keep, mb) + flip(keep, ma | mb)
            keep = near + far
            rest = rest[2:]
    other = flip(keep, 1)
    first = jnp.where(low, keep, other)
    second = jnp.where(low, other, keep)
    return unpack(first, second)


def bounded_cos(x):
    k = jnp.round(x * (1.0 / math.pi))
    r = x - k * 3.140625
    r = r - k * 0.0009676535846665502
    r2 = r * r
    poly = -1.0 / 479001600.0 * r2 + 1.0 / 3628800.0
    poly = poly * r2 - 1.0 / 40320.0
    poly = poly * r2 + 1.0 / 720.0
    poly = poly * r2 - 1.0 / 24.0
    poly = poly * r2 + 0.5
    value = 1.0 - poly * r2
    half = k * 0.5
    return jnp.where(jnp.floor(half) == half, value, -value)


def split_gram(f):
    def tdot(a, b):
        return lax.dot_general(a, b, (((0,), (0,)), ((), ())), preferred_element_type=jnp.float32)

    top = lax.reduce_precision(f, exponent_bits=8, mantissa_bits=7)
    rest = f - top
    middle = lax.reduce_precision(rest, exponent_bits=8, mantissa_bits=7)
    high = top.astype(jnp.bfloat16)
    mid = middle.astype(jnp.bfloat16)
    low = (rest - middle).astype(jnp.bfloat16)
    cross = tdot(high, mid) + tdot(high, low)
    return tdot(high, high) + (cross + cross.T) + tdot(mid, mid)


def per_device(inputs, freqs, phases, sample_weight, stored, root):
    total_rows = inputs.shape[0] * lax.axis_size("grp") * lax.axis_size("leaf")
    norm_scale = 1.0 / math.sqrt(total_rows)
    proj = jnp.dot(inputs, freqs, precision=lax.Precision.HIGHEST) + phases[None, :]
    features = jnp.sqrt(sample_weight)[:, None] * bounded_cos(proj) * norm_scale
    slot = lax.axis_index("grp") * lax.axis_size("leaf") + lax.axis_index("leaf")
    running = jnp.where(slot == root[0], stored[0], jnp.zeros_like(stored[0]))
    gram = split_gram(jnp.concatenate([features, running], axis=0))
    gram = all_reduce_symmetric(gram)
    lower, inverse = cholesky_and_inverse(*gram)
    basis = lax.dot_general(
        features, inverse, (((1,), (1,)), ((), ())), precision=lax.Precision.HIGHEST
    ) * math.sqrt(total_rows)
    return (lower.T, basis)


def solution(mesh):
    return jax.shard_map(
        per_device,
        mesh=mesh,
        in_specs=(
            P(("grp", "leaf"), None),
            P(),
            P(),
            P(("grp", "leaf")),
            P(("grp", "leaf"), None, None),
            P(),
        ),
        out_specs=(P(), P(("grp", "leaf"), None)),
        check_vma=False,
    )
```

```python
import math

import jax
import jax.numpy as jnp
from jax import lax
from jax.sharding import PartitionSpec as P


def partner(array, axis, distance):
    return lax.ppermute(array, axis, [(i, i ^ 1 << distance) for i in range(lax.axis_size(axis))])


def mm(a, b):
    return jnp.dot(a, b, precision=lax.Precision.HIGHEST)


def shared_inverse(lower):
    q = lower.shape[0] // 2
    low = (lax.axis_index("grp") * lax.axis_size("leaf") + lax.axis_index("leaf")) % 2 == 0
    block = jnp.where(low, lower[:q, :q], lower[q:, q:])
    mine = lax.linalg.triangular_solve(
        block, jnp.eye(q, dtype=lower.dtype), left_side=True, lower=True
    )
    other = flip(mine, 1)
    top = jnp.where(low, mine, other)
    bottom = jnp.where(low, other, mine)
    corner = -mm(bottom, mm(lower[q:, :q], top))
    zero = jnp.zeros_like(top)
    return jnp.block([[top, zero], [corner, bottom]])


def cholesky_and_inverse(g11, g21, g22):
    l11 = lax.linalg.cholesky(g11, symmetrize_input=False)
    i11 = shared_inverse(l11)
    l21 = mm(g21, i11.T)
    l22 = lax.linalg.cholesky(g22 - mm(l21, l21.T), symmetrize_input=False)
    i22 = shared_inverse(l22)
    i21 = -mm(i22, mm(l21, i11))
    zero = jnp.zeros_like(l11)
    lower = jnp.block([[l11, zero], [l21, l22]])
    inverse = jnp.block([[i11, zero], [i21, i22]])
    return lower, inverse


def pack(gram):
    h = gram.shape[0] // 2
    row = lax.broadcasted_iota(jnp.int32, (h, h), 0)
    col = lax.broadcasted_iota(jnp.int32, (h, h), 1)
    tri = jnp.where(row <= col, gram[:h, :h], gram[h:, h:])
    diag = jnp.sum(jnp.where(row == col, gram[h:, h:], 0.0), axis=0)
    pad = jnp.zeros((7, h), gram.dtype)
    first = jnp.concatenate([tri, diag[None, :], pad], axis=0)
    second = jnp.concatenate([gram[h:, :h], jnp.zeros((8, h), gram.dtype)], axis=0)
    return first, second


def unpack(first, second):
    h = first.shape[1]
    row = lax.broadcasted_iota(jnp.int32, (h, h), 0)
    col = lax.broadcasted_iota(jnp.int32, (h, h), 1)
    tri = first[:h]
    g11 = jnp.where(row <= col, tri, tri.T)
    g22 = jnp.where(row > col, tri, tri.T)
    g22 = jnp.where(row == col, first[h:h + 1, :], g22)
    g21 = second[:h]
    return g11, g21, g22


def flip(array, mask):
    axes = ("grp", "leaf")
    count = lax.axis_size("grp") * lax.axis_size("leaf")
    return lax.ppermute(array, axes, [(i, i ^ mask) for i in range(count)])


def all_reduce_symmetric(gram):
    bits = (lax.axis_size("grp") * lax.axis_size("leaf")).bit_length() - 1
    first, second = pack(gram)
    if bits == 0:
        return unpack(first, second)
    me = lax.axis_index("grp") * lax.axis_size("leaf") + lax.axis_index("leaf")
    low = me % 2 == 0
    keep = jnp.where(low, first, second)
    send = jnp.where(low, second, first)
    keep = keep + flip(send, 1)
    rest = list(range(1, bits))
    while rest:
        if len(rest) == 1:
            keep = keep + flip(keep, 1 << rest[0])
            rest = []
        else:
            ma, mb = 1 << rest[0], 1 << rest[1]
            near = keep + flip(keep, ma)
            far = flip(keep, mb) + flip(keep, ma | mb)
            keep = near + far
            rest = rest[2:]
    other = flip(keep, 1)
    first = jnp.where(low, keep, other)
    second = jnp.where(low, other, keep)
    return unpack(first, second)


def bounded_cos(x):
    k = jnp.round(x * (1.0 / math.pi))
    r = x - k * 3.140625
    r = r - k * 0.0009676535846665502
    r2 = r * r
    poly = -2.61909292476048e-07 * r2 + 2.4769165975158103e-05
    poly = poly * r2 - 0.0013888566754758358
    poly = poly * r2 + 0.041666656732559204
    poly = poly * r2 - 0.5
    value = poly * r2 + 1.0
    half = k * 0.5
    return jnp.where(jnp.floor(half) == half, value, -value)


def split_gram(f):
    def tdot(a, b):
        return lax.dot_general(a, b, (((0,), (0,)), ((), ())), preferred_element_type=jnp.float32)

    top = lax.reduce_precision(f, exponent_bits=8, mantissa_bits=7)
    rest = f - top
    middle = lax.reduce_precision(rest, exponent_bits=8, mantissa_bits=7)
    high = top.astype(jnp.bfloat16)
    mid = middle.astype(jnp.bfloat16)
    low = (rest - middle).astype(jnp.bfloat16)
    cross = tdot(high, mid) + tdot(high, low)
    return tdot(high, high) + (cross + cross.T) + tdot(mid, mid)


def per_device(inputs, freqs, phases, sample_weight, stored, root):
    total_rows = inputs.shape[0] * lax.axis_size("grp") * lax.axis_size("leaf")
    norm_scale = 1.0 / math.sqrt(total_rows)
    proj = jnp.dot(inputs, freqs, precision=lax.Precision.HIGHEST) + phases[None, :]
    features = jnp.sqrt(sample_weight)[:, None] * bounded_cos(proj) * norm_scale
    slot = lax.axis_index("grp") * lax.axis_size("leaf") + lax.axis_index("leaf")
    running = jnp.where(slot == root[0], stored[0], jnp.zeros_like(stored[0]))
    gram = split_gram(jnp.concatenate([features, running], axis=0))
    gram = all_reduce_symmetric(gram)
    lower, inverse = cholesky_and_inverse(*gram)
    basis = lax.dot_general(
        features, inverse, (((1,), (1,)), ((), ())), precision=lax.Precision.HIGHEST
    ) * math.sqrt(total_rows)
    return (lower.T, basis)


def solution(mesh):
    return jax.shard_map(
        per_device,
        mesh=mesh,
        in_specs=(
            P(("grp", "leaf"), None),
            P(),
            P(),
            P(("grp", "leaf")),
            P(("grp", "leaf"), None, None),
            P(),
        ),
        out_specs=(P(), P(("grp", "leaf"), None)),
        check_vma=False,
    )
```

```python
import math

import jax
import jax.numpy as jnp
from jax import lax
from jax.sharding import PartitionSpec as P


def partner(array, axis, distance):
    return lax.ppermute(array, axis, [(i, i ^ 1 << distance) for i in range(lax.axis_size(axis))])


def mm(a, b):
    return jnp.dot(a, b, precision=lax.Precision.HIGHEST)


def shared_inverse(lower):
    q = lower.shape[0] // 2
    low = (lax.axis_index("grp") * lax.axis_size("leaf") + lax.axis_index("leaf")) % 2 == 0
    block = jnp.where(low, lower[:q, :q], lower[q:, q:])
    mine = lax.linalg.triangular_solve(
        block, jnp.eye(q, dtype=lower.dtype), left_side=True, lower=True
    )
    other = flip(mine, 1)
    top = jnp.where(low, mine, other)
    bottom = jnp.where(low, other, mine)
    corner = -mm(bottom, mm(lower[q:, :q], top))
    zero = jnp.zeros_like(top)
    return jnp.block([[top, zero], [corner, bottom]])


def cholesky_and_inverse(g11, g21, g22):
    l11 = lax.linalg.cholesky(g11, symmetrize_input=False)
    i11 = shared_inverse(l11)
    l21 = mm(g21, i11.T)
    l22 = lax.linalg.cholesky(g22 - mm(l21, l21.T), symmetrize_input=False)
    i22 = shared_inverse(l22)
    i21 = -mm(i22, mm(l21, i11))
    zero = jnp.zeros_like(l11)
    lower = jnp.block([[l11, zero], [l21, l22]])
    inverse = jnp.block([[i11, zero], [i21, i22]])
    return lower, inverse


def pack(gram):
    h = gram.shape[0] // 2
    row = lax.broadcasted_iota(jnp.int32, (h, h), 0)
    col = lax.broadcasted_iota(jnp.int32, (h, h), 1)
    tri = jnp.where(row <= col, gram[:h, :h], gram[h:, h:])
    diag = jnp.sum(jnp.where(row == col, gram[h:, h:], 0.0), axis=0)
    pad = jnp.zeros((7, h), gram.dtype)
    first = jnp.concatenate([tri, diag[None, :], pad], axis=0)
    second = jnp.concatenate([gram[h:, :h], jnp.zeros((8, h), gram.dtype)], axis=0)
    return first, second


def unpack(first, second):
    h = first.shape[1]
    row = lax.broadcasted_iota(jnp.int32, (h, h), 0)
    col = lax.broadcasted_iota(jnp.int32, (h, h), 1)
    tri = first[:h]
    g11 = jnp.where(row <= col, tri, tri.T)
    g22 = jnp.where(row > col, tri, tri.T)
    g22 = jnp.where(row == col, first[h:h + 1, :], g22)
    g21 = second[:h]
    return g11, g21, g22


def flip(array, mask):
    axes = ("grp", "leaf")
    count = lax.axis_size("grp") * lax.axis_size("leaf")
    return lax.ppermute(array, axes, [(i, i ^ mask) for i in range(count)])


def all_reduce_symmetric(gram):
    bits = (lax.axis_size("grp") * lax.axis_size("leaf")).bit_length() - 1
    first, second = pack(gram)
    if bits == 0:
        return unpack(first, second)
    me = lax.axis_index("grp") * lax.axis_size("leaf") + lax.axis_index("leaf")
    low = me % 2 == 0
    keep = jnp.where(low, first, second)
    send = jnp.where(low, second, first)
    keep = keep + flip(send, 1)
    rest = list(range(1, bits))
    while rest:
        if len(rest) == 1:
            keep = keep + flip(keep, 1 << rest[0])
            rest = []
        else:
            ma, mb = 1 << rest[0], 1 << rest[1]
            near = keep + flip(keep, ma)
            far = flip(keep, mb) + flip(keep, ma | mb)
            keep = near + far
            rest = rest[2:]
    other = flip(keep, 1)
    first = jnp.where(low, keep, other)
    second = jnp.where(low, other, keep)
    return unpack(first, second)


def bounded_cos(x):
    k = jnp.round(x * (1.0 / math.pi))
    r = x - k * 3.140625
    r = r - k * 0.0009676535846665502
    r2 = r * r
    poly = -2.61909292476048e-07 * r2 + 2.4769165975158103e-05
    poly = poly * r2 - 0.0013888566754758358
    poly = poly * r2 + 0.041666656732559204
    poly = poly * r2 - 0.5
    value = poly * r2 + 1.0
    half = k * 0.5
    return jnp.where(jnp.floor(half) == half, value, -value)


def split_gram(f):
    def tdot(a, b):
        return lax.dot_general(a, b, (((0,), (0,)), ((), ())), preferred_element_type=jnp.float32)

    top = lax.reduce_precision(f, exponent_bits=8, mantissa_bits=7)
    rest = f - top
    middle = lax.reduce_precision(rest, exponent_bits=8, mantissa_bits=7)
    high = top.astype(jnp.bfloat16)
    mid = middle.astype(jnp.bfloat16)
    low = (rest - middle).astype(jnp.bfloat16)
    cross = tdot(high, mid) + tdot(high, low)
    return tdot(high, high) + (cross + cross.T) + tdot(mid, mid)


def per_device(inputs, freqs, phases, sample_weight, stored, root):
    total_rows = inputs.shape[0] * lax.axis_size("grp") * lax.axis_size("leaf")
    norm_scale = 1.0 / math.sqrt(total_rows)
    proj = jnp.dot(inputs, freqs, precision=lax.Precision.HIGHEST) + phases[None, :]
    features = (jnp.sqrt(sample_weight) * norm_scale)[:, None] * bounded_cos(proj)
    slot = lax.axis_index("grp") * lax.axis_size("leaf") + lax.axis_index("leaf")
    running = jnp.where(slot == root[0], stored[0], jnp.zeros_like(stored[0]))
    gram = split_gram(jnp.concatenate([features, running], axis=0))
    gram = all_reduce_symmetric(gram)
    lower, inverse = cholesky_and_inverse(*gram)
    basis = lax.dot_general(
        features, inverse, (((1,), (1,)), ((), ())), precision=lax.Precision.HIGHEST
    ) * math.sqrt(total_rows)
    return (lower.T, basis)


def solution(mesh):
    return jax.shard_map(
        per_device,
        mesh=mesh,
        in_specs=(
            P(("grp", "leaf"), None),
            P(),
            P(),
            P(("grp", "leaf")),
            P(("grp", "leaf"), None, None),
            P(),
        ),
        out_specs=(P(), P(("grp", "leaf"), None)),
        check_vma=False,
    )
```

```python
import math

import jax
import jax.numpy as jnp
from jax import lax
from jax.sharding import PartitionSpec as P


def partner(array, axis, distance):
    return lax.ppermute(array, axis, [(i, i ^ 1 << distance) for i in range(lax.axis_size(axis))])


def mm(a, b):
    return jnp.dot(a, b, precision=lax.Precision.HIGHEST)


def shared_inverse(lower):
    q = lower.shape[0] // 2
    low = (lax.axis_index("grp") * lax.axis_size("leaf") + lax.axis_index("leaf")) % 2 == 0
    block = jnp.where(low, lower[:q, :q], lower[q:, q:])
    mine = lax.linalg.triangular_solve(
        block, jnp.eye(q, dtype=lower.dtype), left_side=True, lower=True
    )
    other = flip(mine, 1)
    top = jnp.where(low, mine, other)
    bottom = jnp.where(low, other, mine)
    corner = -mm(bottom, mm(lower[q:, :q], top))
    zero = jnp.zeros_like(top)
    return jnp.block([[top, zero], [corner, bottom]])


def cholesky_and_inverse(g11, g21, g22):
    l11 = lax.linalg.cholesky(g11, symmetrize_input=False)
    i11 = shared_inverse(l11)
    l21 = mm(g21, i11.T)
    l22 = lax.linalg.cholesky(g22 - mm(l21, l21.T), symmetrize_input=False)
    i22 = shared_inverse(l22)
    i21 = -mm(i22, mm(l21, i11))
    zero = jnp.zeros_like(l11)
    lower = jnp.block([[l11, zero], [l21, l22]])
    inverse = jnp.block([[i11, zero], [i21, i22]])
    return lower, inverse


def pack(gram):
    h = gram.shape[0] // 2
    row = lax.broadcasted_iota(jnp.int32, (h, h), 0)
    col = lax.broadcasted_iota(jnp.int32, (h, h), 1)
    tri = jnp.where(row <= col, gram[:h, :h], gram[h:, h:])
    diag = jnp.sum(jnp.where(row == col, gram[h:, h:], 0.0), axis=0)
    pad = jnp.zeros((7, h), gram.dtype)
    first = jnp.concatenate([tri, diag[None, :], pad], axis=0)
    second = jnp.concatenate([gram[h:, :h], jnp.zeros((8, h), gram.dtype)], axis=0)
    return first, second


def unpack(first, second):
    h = first.shape[1]
    row = lax.broadcasted_iota(jnp.int32, (h, h), 0)
    col = lax.broadcasted_iota(jnp.int32, (h, h), 1)
    tri = first[:h]
    g11 = jnp.where(row <= col, tri, tri.T)
    g22 = jnp.where(row > col, tri, tri.T)
    g22 = jnp.where(row == col, first[h:h + 1, :], g22)
    g21 = second[:h]
    return g11, g21, g22


def flip(array, mask):
    axes = ("grp", "leaf")
    count = lax.axis_size("grp") * lax.axis_size("leaf")
    return lax.ppermute(array, axes, [(i, i ^ mask) for i in range(count)])


def all_reduce_symmetric(gram):
    bits = (lax.axis_size("grp") * lax.axis_size("leaf")).bit_length() - 1
    first, second = pack(gram)
    if bits == 0:
        return unpack(first, second)
    me = lax.axis_index("grp") * lax.axis_size("leaf") + lax.axis_index("leaf")
    low = me % 2 == 0
    keep = jnp.where(low, first, second)
    send = jnp.where(low, second, first)
    keep = keep + flip(send, 1)
    rest = list(range(1, bits))
    while rest:
        if len(rest) == 1:
            keep = keep + flip(keep, 1 << rest[0])
            rest = []
        else:
            ma, mb = 1 << rest[0], 1 << rest[1]
            near = keep + flip(keep, ma)
            far = flip(keep, mb) + flip(keep, ma | mb)
            keep = near + far
            rest = rest[2:]
    other = flip(keep, 1)
    first = jnp.where(low, keep, other)
    second = jnp.where(low, other, keep)
    return unpack(first, second)


def bounded_cos(x):
    k = jnp.round(x * (0.5 / math.pi))
    r = x - k * 6.28125
    r = r - k * 0.0019353071693331003
    r2 = r * r
    poly = -2.557707934336406e-10 * r2 + 9.675455459046134e-08
    poly = poly * r2 + -2.1700885554309934e-05
    poly = poly * r2 + 0.0026041660457849503
    poly = poly * r2 + -0.125
    half = poly * r2 + 1.0
    return 2.0 * (half * half) - 1.0


def split_gram(f):
    def tdot(a, b):
        return lax.dot_general(a, b, (((0,), (0,)), ((), ())), preferred_element_type=jnp.float32)

    top = lax.reduce_precision(f, exponent_bits=8, mantissa_bits=7)
    rest = f - top
    middle = lax.reduce_precision(rest, exponent_bits=8, mantissa_bits=7)
    high = top.astype(jnp.bfloat16)
    mid = middle.astype(jnp.bfloat16)
    low = (rest - middle).astype(jnp.bfloat16)
    cross = tdot(high, mid) + tdot(high, low)
    return tdot(high, high) + (cross + cross.T) + tdot(mid, mid)


def per_device(inputs, freqs, phases, sample_weight, stored, root):
    total_rows = inputs.shape[0] * lax.axis_size("grp") * lax.axis_size("leaf")
    norm_scale = 1.0 / math.sqrt(total_rows)
    proj = jnp.dot(inputs, freqs, precision=lax.Precision.HIGHEST) + phases[None, :]
    features = (jnp.sqrt(sample_weight) * norm_scale)[:, None] * bounded_cos(proj)
    slot = lax.axis_index("grp") * lax.axis_size("leaf") + lax.axis_index("leaf")
    running = jnp.where(slot == root[0], stored[0], jnp.zeros_like(stored[0]))
    gram = split_gram(jnp.concatenate([features, running], axis=0))
    gram = all_reduce_symmetric(gram)
    lower, inverse = cholesky_and_inverse(*gram)
    basis = lax.dot_general(
        features, inverse, (((1,), (1,)), ((), ())), precision=lax.Precision.HIGHEST
    ) * math.sqrt(total_rows)
    return (lower.T, basis)


def solution(mesh):
    return jax.shard_map(
        per_device,
        mesh=mesh,
        in_specs=(
            P(("grp", "leaf"), None),
            P(),
            P(),
            P(("grp", "leaf")),
            P(("grp", "leaf"), None, None),
            P(),
        ),
        out_specs=(P(), P(("grp", "leaf"), None)),
        check_vma=False,
    )
```

```python
import math

import jax
import jax.numpy as jnp
from jax import lax
from jax.sharding import PartitionSpec as P


def partner(array, axis, distance):
    return lax.ppermute(array, axis, [(i, i ^ 1 << distance) for i in range(lax.axis_size(axis))])


def mm(a, b):
    return jnp.dot(a, b, precision=lax.Precision.HIGHEST)


def shared_inverse(lower):
    q = lower.shape[0] // 2
    low = (lax.axis_index("grp") * lax.axis_size("leaf") + lax.axis_index("leaf")) % 2 == 0
    block = jnp.where(low, lower[:q, :q], lower[q:, q:])
    mine = lax.linalg.triangular_solve(
        block, jnp.eye(q, dtype=lower.dtype), left_side=True, lower=True
    )
    other = flip(mine, 1)
    top = jnp.where(low, mine, other)
    bottom = jnp.where(low, other, mine)
    corner = -mm(bottom, mm(lower[q:, :q], top))
    zero = jnp.zeros_like(top)
    return jnp.block([[top, zero], [corner, bottom]])


def cholesky_and_inverse(g11, g21, g22):
    l11 = lax.linalg.cholesky(g11, symmetrize_input=False)
    i11 = shared_inverse(l11)
    l21 = mm(g21, i11.T)
    l22 = lax.linalg.cholesky(g22 - mm(l21, l21.T), symmetrize_input=False)
    i22 = shared_inverse(l22)
    i21 = -mm(i22, mm(l21, i11))
    zero = jnp.zeros_like(l11)
    lower = jnp.block([[l11, zero], [l21, l22]])
    inverse = jnp.block([[i11, zero], [i21, i22]])
    return lower, inverse


def pack(gram):
    h = gram.shape[0] // 2
    row = lax.broadcasted_iota(jnp.int32, (h, h), 0)
    col = lax.broadcasted_iota(jnp.int32, (h, h), 1)
    tri = jnp.where(row <= col, gram[:h, :h], gram[h:, h:])
    diag = jnp.sum(jnp.where(row == col, gram[h:, h:], 0.0), axis=0)
    pad = jnp.zeros((7, h), gram.dtype)
    first = jnp.concatenate([tri, diag[None, :], pad], axis=0)
    second = jnp.concatenate([gram[h:, :h], jnp.zeros((8, h), gram.dtype)], axis=0)
    return first, second


def unpack(first, second):
    h = first.shape[1]
    row = lax.broadcasted_iota(jnp.int32, (h, h), 0)
    col = lax.broadcasted_iota(jnp.int32, (h, h), 1)
    tri = first[:h]
    g11 = jnp.where(row <= col, tri, tri.T)
    g22 = jnp.where(row > col, tri, tri.T)
    g22 = jnp.where(row == col, first[h:h + 1, :], g22)
    g21 = second[:h]
    return g11, g21, g22


def flip(array, mask):
    axes = ("grp", "leaf")
    count = lax.axis_size("grp") * lax.axis_size("leaf")
    return lax.ppermute(array, axes, [(i, i ^ mask) for i in range(count)])


def all_reduce_symmetric(gram):
    bits = (lax.axis_size("grp") * lax.axis_size("leaf")).bit_length() - 1
    first, second = pack(gram)
    if bits == 0:
        return unpack(first, second)
    me = lax.axis_index("grp") * lax.axis_size("leaf") + lax.axis_index("leaf")
    low = me % 2 == 0
    keep = jnp.where(low, first, second)
    send = jnp.where(low, second, first)
    keep = keep + flip(send, 1)
    rest = list(range(1, bits))
    while rest:
        if len(rest) == 1:
            keep = keep + flip(keep, 1 << rest[0])
            rest = []
        else:
            ma, mb = 1 << rest[0], 1 << rest[1]
            far = flip(keep, ma | mb) + flip(keep, mb)
            near = flip(keep, ma) + keep
            keep = far + near
            rest = rest[2:]
    other = flip(keep, 1)
    first = jnp.where(low, keep, other)
    second = jnp.where(low, other, keep)
    return unpack(first, second)


def bounded_cos(x):
    k = jnp.round(x * (1.0 / math.pi))
    r = x - k * 3.140625
    r = r - k * 0.0009676535846665502
    r2 = r * r
    poly = -2.61909292476048e-07 * r2 + 2.4769165975158103e-05
    poly = poly * r2 - 0.0013888566754758358
    poly = poly * r2 + 0.041666656732559204
    poly = poly * r2 - 0.5
    value = poly * r2 + 1.0
    half = k * 0.5
    return jnp.where(jnp.floor(half) == half, value, -value)


def split_gram(f):
    def tdot(a, b):
        return lax.dot_general(a, b, (((0,), (0,)), ((), ())), preferred_element_type=jnp.float32)

    top = lax.reduce_precision(f, exponent_bits=8, mantissa_bits=7)
    rest = f - top
    middle = lax.reduce_precision(rest, exponent_bits=8, mantissa_bits=7)
    high = top.astype(jnp.bfloat16)
    mid = middle.astype(jnp.bfloat16)
    low = (rest - middle).astype(jnp.bfloat16)
    cross = tdot(high, mid) + tdot(high, low)
    return tdot(high, high) + (cross + cross.T) + tdot(mid, mid)


def per_device(inputs, freqs, phases, sample_weight, stored, root):
    total_rows = inputs.shape[0] * lax.axis_size("grp") * lax.axis_size("leaf")
    norm_scale = 1.0 / math.sqrt(total_rows)
    proj = jnp.dot(inputs, freqs, precision=lax.Precision.HIGHEST) + phases[None, :]
    features = (jnp.sqrt(sample_weight) * norm_scale)[:, None] * bounded_cos(proj)
    slot = lax.axis_index("grp") * lax.axis_size("leaf") + lax.axis_index("leaf")
    running = jnp.where(slot == root[0], stored[0], jnp.zeros_like(stored[0]))
    gram = split_gram(jnp.concatenate([features, running], axis=0))
    gram = all_reduce_symmetric(gram)
    lower, inverse = cholesky_and_inverse(*gram)
    basis = lax.dot_general(
        features, inverse, (((1,), (1,)), ((), ())), precision=lax.Precision.HIGHEST
    ) * math.sqrt(total_rows)
    return (lower.T, basis)


def solution(mesh):
    return jax.shard_map(
        per_device,
        mesh=mesh,
        in_specs=(
            P(("grp", "leaf"), None),
            P(),
            P(),
            P(("grp", "leaf")),
            P(("grp", "leaf"), None, None),
            P(),
        ),
        out_specs=(P(), P(("grp", "leaf"), None)),
        check_vma=False,
    )
```

```python
import math

import jax
import jax.numpy as jnp
from jax import lax
from jax.sharding import PartitionSpec as P


def partner(array, axis, distance):
    return lax.ppermute(array, axis, [(i, i ^ 1 << distance) for i in range(lax.axis_size(axis))])


def mm(a, b):
    return jnp.dot(a, b, precision=lax.Precision.HIGHEST)


def shared_inverse(lower):
    q = lower.shape[0] // 2
    low = (lax.axis_index("grp") * lax.axis_size("leaf") + lax.axis_index("leaf")) % 2 == 0
    block = jnp.where(low, lower[:q, :q], lower[q:, q:])
    mine = lax.linalg.triangular_solve(
        block, jnp.eye(q, dtype=lower.dtype), left_side=True, lower=True
    )
    other = flip(mine, 1)
    top = jnp.where(low, mine, other)
    bottom = jnp.where(low, other, mine)
    corner = -mm(bottom, mm(lower[q:, :q], top))
    zero = jnp.zeros_like(top)
    return jnp.block([[top, zero], [corner, bottom]])


def cholesky_and_inverse(g11, g21, g22):
    l11 = lax.linalg.cholesky(g11, symmetrize_input=False)
    i11 = shared_inverse(l11)
    l21 = mm(g21, i11.T)
    l22 = lax.linalg.cholesky(g22 - mm(l21, l21.T), symmetrize_input=False)
    i22 = shared_inverse(l22)
    i21 = -mm(i22, mm(l21, i11))
    zero = jnp.zeros_like(l11)
    lower = jnp.block([[l11, zero], [l21, l22]])
    inverse = jnp.block([[i11, zero], [i21, i22]])
    return lower, inverse


def pack(gram):
    h = gram.shape[0] // 2
    row = lax.broadcasted_iota(jnp.int32, (h, h), 0)
    col = lax.broadcasted_iota(jnp.int32, (h, h), 1)
    tri = jnp.where(row <= col, gram[:h, :h], gram[h:, h:])
    diag = jnp.sum(jnp.where(row == col, gram[h:, h:], 0.0), axis=0)
    pad = jnp.zeros((7, h), gram.dtype)
    first = jnp.concatenate([tri, diag[None, :], pad], axis=0)
    second = jnp.concatenate([gram[h:, :h], jnp.zeros((8, h), gram.dtype)], axis=0)
    return first, second


def unpack(first, second):
    h = first.shape[1]
    row = lax.broadcasted_iota(jnp.int32, (h, h), 0)
    col = lax.broadcasted_iota(jnp.int32, (h, h), 1)
    tri = first[:h]
    g11 = jnp.where(row <= col, tri, tri.T)
    g22 = jnp.where(row > col, tri, tri.T)
    g22 = jnp.where(row == col, first[h:h + 1, :], g22)
    g21 = second[:h]
    return g11, g21, g22


def flip(array, mask):
    axes = ("grp", "leaf")
    count = lax.axis_size("grp") * lax.axis_size("leaf")
    return lax.ppermute(array, axes, [(i, i ^ mask) for i in range(count)])


def all_reduce_symmetric(gram):
    bits = (lax.axis_size("grp") * lax.axis_size("leaf")).bit_length() - 1
    first, second = pack(gram)
    if bits == 0:
        return unpack(first, second)
    me = lax.axis_index("grp") * lax.axis_size("leaf") + lax.axis_index("leaf")
    low = me % 2 == 0
    keep = jnp.where(low, first, second)
    send = jnp.where(low, second, first)
    keep = keep + flip(send, 1)
    rest = list(range(1, bits))
    while rest:
        if len(rest) == 1:
            keep = keep + flip(keep, 1 << rest[0])
            rest = []
        else:
            ma, mb = 1 << rest[0], 1 << rest[1]
            near = keep + flip(keep, ma)
            far = flip(keep, mb) + flip(keep, ma | mb)
            keep = near + far
            rest = rest[2:]
    other = flip(keep, 1)
    first = jnp.where(low, keep, other)
    second = jnp.where(low, other, keep)
    return unpack(first, second)


def bounded_cos(x):
    k = jnp.round(x * (1.0 / math.pi))
    r = x - k * 3.140625
    r = r - k * 0.0009676535846665502
    r2 = r * r
    poly = -2.61909292476048e-07 * r2 + 2.4769165975158103e-05
    poly = poly * r2 - 0.0013888566754758358
    poly = poly * r2 + 0.041666656732559204
    poly = poly * r2 - 0.5
    value = poly * r2 + 1.0
    half = k * 0.5
    return jnp.where(jnp.floor(half) == half, value, -value)


def split_gram(f):
    def tdot(a, b):
        return lax.dot_general(a, b, (((0,), (0,)), ((), ())), preferred_element_type=jnp.float32)

    top = lax.reduce_precision(f, exponent_bits=8, mantissa_bits=7)
    rest = f - top
    middle = lax.reduce_precision(rest, exponent_bits=8, mantissa_bits=7)
    high = top.astype(jnp.bfloat16)
    mid = middle.astype(jnp.bfloat16)
    low = (rest - middle).astype(jnp.bfloat16)
    cross = tdot(high, mid) + tdot(high, low)
    return tdot(high, high) + (cross + cross.T) + tdot(mid, mid)


def per_device(inputs, freqs, phases, sample_weight, stored, root):
    total_rows = inputs.shape[0] * lax.axis_size("grp") * lax.axis_size("leaf")
    norm_scale = 1.0 / math.sqrt(total_rows)
    proj = jnp.dot(inputs, freqs, precision=lax.Precision.HIGHEST) + phases[None, :]
    features = (jnp.sqrt(sample_weight) * norm_scale)[:, None] * bounded_cos(proj)
    slot = lax.axis_index("grp") * lax.axis_size("leaf") + lax.axis_index("leaf")
    running = jnp.where(slot == root[0], stored[0], jnp.zeros_like(stored[0]))
    gram = split_gram(jnp.concatenate([features, running], axis=0))
    gram = all_reduce_symmetric(gram)
    lower, inverse = cholesky_and_inverse(*gram)
    basis = lax.dot_general(
        features, inverse * math.sqrt(total_rows), (((1,), (1,)), ((), ())),
        precision=lax.Precision.HIGHEST,
    )
    return (lower.T, basis)


def solution(mesh):
    return jax.shard_map(
        per_device,
        mesh=mesh,
        in_specs=(
            P(("grp", "leaf"), None),
            P(),
            P(),
            P(("grp", "leaf")),
            P(("grp", "leaf"), None, None),
            P(),
        ),
        out_specs=(P(), P(("grp", "leaf"), None)),
        check_vma=False,
    )
```
